512 devices in a mesh: gx: 32 (over z, core), gy: 16 (over x, y).
Axes of the slice: x: 4, y: 4, z: 16, core: 2. Of those that a mesh axis runs over, the one named last changes fastest.
Arguments:
- field: bfloat16 [1024, 65536], P('gx', 'gy'), may hold values from -6 to 6
- dw0: float32 [9, 32], replicated, may hold values from -2 to 2
- pw0: bfloat16 [32, 32], replicated, may hold values from -1.5 to 1.5
- dw1: float32 [9, 32], replicated, may hold values from -2 to 2
- pw1: bfloat16 [32, 64], replicated, may hold values from -1.5 to 1.5
- dw2: float32 [9, 64], replicated, may hold values from -2 to 2
- pw2: bfloat16 [64, 128], replicated, may hold values from -1 to 1
- dw3: float32 [9, 128], replicated, may hold values from -2 to 2
- pw3: bfloat16 [128, 256], replicated, may hold values from -0.75 to 0.75
- dw4: float32 [9, 256], replicated, may hold values from -2 to 2
- pw4: bfloat16 [256, 512], replicated, may hold values from -0.5 to 0.5
- dwc: float32 [4, 9, 512], replicated, may hold values from -2 to 2
- pwc: bfloat16 [4, 512, 512], replicated, may hold values from -0.375 to 0.375
Outputs:
- fine: bfloat16 [1024, 65536], P('gx', 'gy')
- coarse: bfloat16 [4, 4096], replicated
The draws below stay inside these ranges and needn't reach their ends.
All inputs are finite; a program needn't handle non-finite values.
Results may differ from the reference program's by a relative error of at most 0.024.
Values may be sent and summed in bfloat16 or wider, within the bound.
No kernel may reach another device: no remote copies, remote signals or barrier semaphores. Data moves between devices by JAX's collectives and lax.ppermute only.
A program may use at most 64 MiB of HBM per device.

```python
import jax
import jax.numpy as jnp

C0 = 32
CT = 512
LC = 4
NX = 1024
NY = 2048


def levels(key, extent, shards, least, top_value):
    def one(axis_at, parts):
        heights = jax.random.uniform(jax.random.fold_in(jax.random.fold_in(key, 6), axis_at), (parts,), jnp.float32, least / len(shards), top_value / len(shards))
        return jnp.repeat(jnp.exp(heights), extent[axis_at] // parts).reshape((-1,) + (1,) * (len(extent) - axis_at - 1))

    level = one(*shards[0])
    for cut in shards[1:]:
        level = level * one(*cut)
    return level


def gaussian(own_key, shape, scale, limit, pieces=(), kind=jnp.bfloat16):
    entries = jax.random.normal(own_key, shape, jnp.float32) * scale
    if len(pieces) > 0:
        entries = levels(own_key, shape, pieces, -0.22, 0.18) * entries
    return jnp.clip(entries, min=-limit, max=limit).astype(kind)


def setup_inputs(seed: int = 0) -> dict:
    keys = jax.random.split(jax.random.key(seed), 14)
    field = gaussian(keys[0], (NX, NY * C0), 1.0, 6.0, ((0, 32), (1, 16)))
    dw0 = gaussian(keys[1], (9, C0), 0.33, 2.0, (), jnp.float32)
    pw0 = gaussian(keys[2], (C0, C0), (C0 // 2) ** -0.5, 1.5)
    dw1 = gaussian(keys[3], (9, C0), 0.33, 2.0, (), jnp.float32)
    pw1 = gaussian(keys[4], (C0, 2 * C0), (C0 // 2) ** -0.5, 1.5)
    dw2 = gaussian(keys[5], (9, 2 * C0), 0.33, 2.0, (), jnp.float32)
    pw2 = gaussian(keys[6], (2 * C0, 4 * C0), C0 ** -0.5, 1.0)
    dw3 = gaussian(keys[7], (9, 4 * C0), 0.33, 2.0, (), jnp.float32)
    pw3 = gaussian(keys[8], (4 * C0, 8 * C0), (2 * C0) ** -0.5, 0.75)
    dw4 = gaussian(keys[9], (9, 8 * C0), 0.33, 2.0, (), jnp.float32)
    pw4 = gaussian(keys[10], (8 * C0, CT), (4 * C0) ** -0.5, 0.5)
    dwc = gaussian(keys[11], (LC, 9, CT), 0.33, 2.0, (), jnp.float32)
    pwc = gaussian(keys[12], (LC, CT, CT), (CT // 2) ** -0.5, 0.375)
    return {"field": field, "dw0": dw0, "pw0": pw0, "dw1": dw1, "pw1": pw1, "dw2": dw2, "pw2": pw2, "dw3": dw3, "pw3": pw3, "dw4": dw4, "pw4": pw4, "dwc": dwc, "pwc": pwc}


def gelu_tanh(value):
    return jax.nn.gelu(value, approximate=True)


def taps_sum(padded, taps, rows, cols, step, spacing):
    total = jnp.zeros((rows, cols, padded.shape[2]), jnp.float32)
    for first in range(3):
        for second in range(3):
            piece = padded[first * spacing:first * spacing + rows * step:step,
                           second * spacing:second * spacing + cols * step:step]
            total = total + piece.astype(jnp.float32) * taps[3 * first + second]
    return total


def point_mix(spread, weight):
    rows, cols, chans = spread.shape
    flat = spread.astype(jnp.bfloat16).reshape(rows * cols, chans)
    mixed = jnp.dot(flat, weight, preferred_element_type=jnp.float32)
    return gelu_tanh(mixed).reshape(rows, cols, weight.shape[1])


def strided(field, taps, weight):
    rows, cols, chans = field.shape
    padded = jnp.pad(field, ((1, 0), (1, 0), (0, 0)))
    spread = taps_sum(padded, taps, rows // 2, cols // 2, 2, 1)
    return point_mix(spread, weight).astype(jnp.bfloat16)


def reference(field, dw0, pw0, dw1, pw1, dw2, pw2, dw3, pw3, dw4, pw4, dwc, pwc):
    chans = dw0.shape[1]
    grid = field.reshape(field.shape[0], -1, chans)
    padded = jnp.pad(grid, ((2, 2), (2, 2), (0, 0)))
    spread = taps_sum(padded, dw0, grid.shape[0], grid.shape[1], 1, 2)
    hidden = (grid.astype(jnp.float32) + point_mix(spread, pw0)).astype(jnp.bfloat16)
    fine = hidden.reshape(hidden.shape[0], -1)
    for taps, weight in ((dw1, pw1), (dw2, pw2), (dw3, pw3), (dw4, pw4)):
        hidden = strided(hidden, taps, weight)
    for level in range(LC):
        hidden = strided(hidden, dwc[level], pwc[level])
    return (fine, hidden.reshape(hidden.shape[0], -1))
```

```python
import jax
import jax.numpy as jnp
from jax import lax
from jax.sharding import PartitionSpec as P

LC = 4


def shifted(value, axis, steps):
    count = lax.axis_size(axis)
    leading, last = (max(0, -steps), min(count, count - steps))
    return lax.ppermute(value, axis, [(source, source + steps) for source in range(leading, last)])


def padded_2(block, sides, width):
    for axis, dim in sides:
        count = lax.axis_size(axis)
        forward = [(i, i + 1) for i in range(count - 1)]
        backward = [(target, source) for source, target in forward]
        low = lax.ppermute(
            lax.slice_in_dim(block, block.shape[dim] - width, None, axis=dim), axis, forward
        )
        high = lax.ppermute(lax.slice_in_dim(block, 0, width, axis=dim), axis, backward)
        block = jnp.concatenate([low, block, high], axis=dim)
    return block


def gelu_tanh(value):
    return jax.nn.gelu(value, approximate=True)


def point_flat(spread, weight, rows, cols):
    chans = weight.shape[0]
    flat = spread.astype(jnp.bfloat16).reshape(rows * cols, chans)
    mixed = jnp.dot(flat, weight, preferred_element_type=jnp.float32)
    return gelu_tanh(mixed).reshape(rows, cols * weight.shape[1])


def down_level(field, taps, weight, split_rows, split_cols):
    chans = taps.shape[1]
    rows = field.shape[0]
    cols = field.shape[1] // chans
    half_rows = rows // 2
    half_cols = cols // 2
    if split_rows:
        upper = shifted(field[-1:], "gx", 1)
    else:
        upper = jnp.zeros((1, cols * chans), jnp.bfloat16)
    extended = jnp.concatenate([upper, field], axis=0)
    if split_cols:
        leftside = shifted(extended[:, -chans:], "gy", 1)
    else:
        leftside = jnp.zeros((rows + 1, chans), jnp.bfloat16)
    tiled = jnp.tile(taps, (1, half_cols))
    total = jnp.zeros((half_rows, half_cols * chans), jnp.float32)
    for first in range(3):
        slab = extended[first : first + rows : 2]
        left_slab = leftside[first : first + rows : 2]
        pairs = slab.reshape(half_rows, half_cols, 2 * chans)
        even_cells = pairs[:, :, :chans].reshape(half_rows, half_cols * chans)
        odd_cells = pairs[:, :, chans:].reshape(half_rows, half_cols * chans)
        before = jnp.concatenate([left_slab, odd_cells[:, :-chans]], axis=1)
        for second, piece in enumerate((before, even_cells, odd_cells)):
            total = total + piece.astype(jnp.float32) * tiled[3 * first + second]
    return point_flat(total, weight, half_rows, half_cols).astype(jnp.bfloat16)


def local(field, dw0, pw0, dw1, pw1, dw2, pw2, dw3, pw3, dw4, pw4, dwc, pwc):
    chans = dw0.shape[1]
    rows = field.shape[0]
    cols = field.shape[1] // chans
    grid = field.reshape(rows, cols, chans)
    padded = padded_2(grid, (("gx", 0), ("gy", 1)), 2)
    flat_pad = padded.reshape(rows + 4, (cols + 4) * chans)
    tiled = jnp.tile(dw0, (1, cols))
    total = jnp.zeros((rows, cols * chans), jnp.float32)
    for first in range(3):
        for second in range(3):
            piece = flat_pad[
                2 * first : 2 * first + rows, 2 * second * chans : 2 * second * chans + cols * chans
            ]
            total = total + piece.astype(jnp.float32) * tiled[3 * first + second]
    hidden = (field.astype(jnp.float32) + point_flat(total, pw0, rows, cols)).astype(jnp.bfloat16)
    fine = hidden
    for taps, weight in ((dw1, pw1), (dw2, pw2), (dw3, pw3), (dw4, pw4)):
        hidden = down_level(hidden, taps, weight, True, True)
    coarse_chans = dwc.shape[2]
    halo = 2 ** (LC - 1) - 1
    grid4 = hidden.reshape(hidden.shape[0], -1, coarse_chans)
    upper = shifted(grid4[-1:], "gx", 1)
    extended = jnp.concatenate([upper, grid4], axis=0)
    leftside = shifted(extended[:, -halo:], "gy", 1)
    extended = jnp.concatenate([leftside, extended], axis=1)
    hidden = strided_cells(extended, dwc[0], pwc[0])
    hidden = lax.all_gather(hidden, "gx", axis=0, tiled=True)
    for level in range(1, LC - 1):
        hidden = strided_cells(pad_top(hidden), dwc[level], pwc[level])
    hidden = lax.all_gather(hidden, "gy", axis=1, tiled=True)
    hidden = strided_cells(pad_left(pad_top(hidden)), dwc[LC - 1], pwc[LC - 1])
    return (fine, hidden.reshape(hidden.shape[0], -1))


def pad_top(cells):
    return jnp.concatenate([jnp.zeros_like(cells[:1]), cells], axis=0)


def pad_left(cells):
    return jnp.concatenate([jnp.zeros_like(cells[:, :1]), cells], axis=1)


def strided_cells(padded, taps, weight):
    rows = (padded.shape[0] - 1) // 2
    cols = (padded.shape[1] - 1) // 2
    total = jnp.zeros((rows, cols, padded.shape[2]), jnp.float32)
    for first in range(3):
        for second in range(3):
            piece = padded[first : first + 2 * rows : 2, second : second + 2 * cols : 2]
            total = total + piece.astype(jnp.float32) * taps[3 * first + second]
    flat = total.astype(jnp.bfloat16).reshape(rows * cols, -1)
    mixed = jnp.dot(flat, weight, preferred_element_type=jnp.float32)
    return gelu_tanh(mixed).astype(jnp.bfloat16).reshape(rows, cols, weight.shape[1])


def solution(mesh):
    placed = (P("gx", "gy"), P(), P(), P(), P(), P(), P(), P(), P(), P(), P(), P(), P())
    return jax.shard_map(
        local, mesh=mesh, in_specs=placed, out_specs=(P("gx", "gy"), P()), check_vma=False
    )
```

```python
import jax
import jax.numpy as jnp
from jax import lax
from jax.sharding import PartitionSpec as P

LC = 4


def shifted(value, axis, steps):
    count = lax.axis_size(axis)
    leading, last = (max(0, -steps), min(count, count - steps))
    return lax.ppermute(value, axis, [(source, source + steps) for source in range(leading, last)])


def padded_2(block, sides, width):
    for axis, dim in sides:
        count = lax.axis_size(axis)
        forward = [(i, i + 1) for i in range(count - 1)]
        backward = [(target, source) for source, target in forward]
        low = lax.ppermute(
            lax.slice_in_dim(block, block.shape[dim] - width, None, axis=dim), axis, forward
        )
        high = lax.ppermute(lax.slice_in_dim(block, 0, width, axis=dim), axis, backward)
        block = jnp.concatenate([low, block, high], axis=dim)
    return block


def gelu_tanh(value):
    return jax.nn.gelu(value, approximate=True)


def point_flat(spread, weight, rows, cols):
    chans = weight.shape[0]
    flat = spread.astype(jnp.bfloat16).reshape(rows * cols, chans)
    mixed = jnp.dot(flat, weight, preferred_element_type=jnp.float32)
    return gelu_tanh(mixed).reshape(rows, cols * weight.shape[1])


def down_level(field, taps, weight, split_rows, split_cols):
    chans = taps.shape[1]
    rows = field.shape[0]
    cols = field.shape[1] // chans
    half_rows = rows // 2
    half_cols = cols // 2
    if split_rows:
        upper = shifted(field[-1:], "gx", 1)
    else:
        upper = jnp.zeros((1, cols * chans), jnp.bfloat16)
    extended = jnp.concatenate([upper, field], axis=0)
    if split_cols:
        leftside = shifted(extended[:, -chans:], "gy", 1)
    else:
        leftside = jnp.zeros((rows + 1, chans), jnp.bfloat16)
    tiled = jnp.tile(taps, (1, half_cols))
    total = jnp.zeros((half_rows, half_cols * chans), jnp.float32)
    for first in range(3):
        slab = extended[first : first + rows : 2]
        left_slab = leftside[first : first + rows : 2]
        pairs = slab.reshape(half_rows, half_cols, 2 * chans)
        even_cells = pairs[:, :, :chans].reshape(half_rows, half_cols * chans)
        odd_cells = pairs[:, :, chans:].reshape(half_rows, half_cols * chans)
        before = jnp.concatenate([left_slab, odd_cells[:, :-chans]], axis=1)
        for second, piece in enumerate((before, even_cells, odd_cells)):
            total = total + piece.astype(jnp.float32) * tiled[3 * first + second]
    return point_flat(total, weight, half_rows, half_cols).astype(jnp.bfloat16)


def strided_flat(ext, taps, weight):
    chans = taps.shape[1]
    rows = (ext.shape[0] - 1) // 2
    cols = (ext.shape[1] // chans - 1) // 2
    tiled = jnp.tile(taps, (1, cols))
    total = jnp.zeros((rows, cols * chans), jnp.float32)
    for first in range(3):
        slab = ext[first : first + 2 * rows : 2]
        head = slab[:, : 2 * cols * chans].reshape(rows, cols, 2 * chans)
        tail = slab[:, chans:].reshape(rows, cols, 2 * chans)
        pieces = (head[:, :, :chans], head[:, :, chans:], tail[:, :, chans:])
        for second, piece in enumerate(pieces):
            piece = piece.reshape(rows, cols * chans)
            total = total + piece.astype(jnp.float32) * tiled[3 * first + second]
    return point_flat(total, weight, rows, cols).astype(jnp.bfloat16)


def local(field, dw0, pw0, dw1, pw1, dw2, pw2, dw3, pw3, dw4, pw4, dwc, pwc):
    chans = dw0.shape[1]
    rows = field.shape[0]
    cols = field.shape[1] // chans
    depth = 4
    margin = 2**depth - 1
    upper = shifted(field[-margin - 2 :], "gx", 1)
    lower = shifted(field[:2], "gx", -1)
    stacked = jnp.concatenate([upper, field, lower], axis=0)
    leftside = shifted(stacked[:, -(margin + 2) * chans :], "gy", 1)
    rightside = shifted(stacked[:, : 2 * chans], "gy", -1)
    flat_pad = jnp.concatenate([leftside, stacked, rightside], axis=1)
    ext_rows = rows + margin
    ext_cols = cols + margin
    tiled = jnp.tile(dw0, (1, ext_cols))
    total = jnp.zeros((ext_rows, ext_cols * chans), jnp.float32)
    for first in range(3):
        for second in range(3):
            piece = flat_pad[
                2 * first : 2 * first + ext_rows,
                2 * second * chans : 2 * second * chans + ext_cols * chans,
            ]
            total = total + piece.astype(jnp.float32) * tiled[3 * first + second]
    centre = flat_pad[2 : 2 + ext_rows, 2 * chans : 2 * chans + ext_cols * chans]
    hidden = (centre.astype(jnp.float32) + point_flat(total, pw0, ext_rows, ext_cols)).astype(
        jnp.bfloat16
    )
    row_ok = (lax.axis_index("gx") > 0) | (lax.broadcasted_iota(jnp.int32, hidden.shape, 0) >= margin)
    col_ok = (lax.axis_index("gy") > 0) | (
        lax.broadcasted_iota(jnp.int32, hidden.shape, 1) >= margin * chans
    )
    hidden = jnp.where(row_ok & col_ok, hidden, jnp.zeros_like(hidden))
    fine = hidden[margin:, margin * chans :]
    for taps, weight in ((dw1, pw1), (dw2, pw2), (dw3, pw3), (dw4, pw4)):
        hidden = strided_flat(hidden, taps, weight)
    coarse_chans = dwc.shape[2]
    halo = 2 ** (LC - 1) - 1
    grid4 = hidden.reshape(hidden.shape[0], -1, coarse_chans)
    upper = shifted(grid4[-1:], "gx", 1)
    extended = jnp.concatenate([upper, grid4], axis=0)
    leftside = shifted(extended[:, -halo:], "gy", 1)
    extended = jnp.concatenate([leftside, extended], axis=1)
    hidden = strided_cells(extended, dwc[0], pwc[0])
    hidden = lax.all_gather(hidden, "gx", axis=0, tiled=True)
    for level in range(1, LC - 1):
        hidden = strided_cells(pad_top(hidden), dwc[level], pwc[level])
    hidden = lax.all_gather(hidden, "gy", axis=1, tiled=True)
    hidden = strided_cells(pad_left(pad_top(hidden)), dwc[LC - 1], pwc[LC - 1])
    return (fine, hidden.reshape(hidden.shape[0], -1))


def pad_top(cells):
    return jnp.concatenate([jnp.zeros_like(cells[:1]), cells], axis=0)


def pad_left(cells):
    return jnp.concatenate([jnp.zeros_like(cells[:, :1]), cells], axis=1)


def strided_cells(padded, taps, weight):
    rows = (padded.shape[0] - 1) // 2
    cols = (padded.shape[1] - 1) // 2
    total = jnp.zeros((rows, cols, padded.shape[2]), jnp.float32)
    for first in range(3):
        for second in range(3):
            piece = padded[first : first + 2 * rows : 2, second : second + 2 * cols : 2]
            total = total + piece.astype(jnp.float32) * taps[3 * first + second]
    flat = total.astype(jnp.bfloat16).reshape(rows * cols, -1)
    mixed = jnp.dot(flat, weight, preferred_element_type=jnp.float32)
    return gelu_tanh(mixed).astype(jnp.bfloat16).reshape(rows, cols, weight.shape[1])


def solution(mesh):
    placed = (P("gx", "gy"), P(), P(), P(), P(), P(), P(), P(), P(), P(), P(), P(), P())
    return jax.shard_map(
        local, mesh=mesh, in_specs=placed, out_specs=(P("gx", "gy"), P()), check_vma=False
    )
```

```python
import jax
import jax.numpy as jnp
from jax import lax
from jax.sharding import PartitionSpec as P

LC = 4


def shifted(value, axis, steps):
    count = lax.axis_size(axis)
    leading, last = (max(0, -steps), min(count, count - steps))
    return lax.ppermute(value, axis, [(source, source + steps) for source in range(leading, last)])


def padded_2(block, sides, width):
    for axis, dim in sides:
        count = lax.axis_size(axis)
        forward = [(i, i + 1) for i in range(count - 1)]
        backward = [(target, source) for source, target in forward]
        low = lax.ppermute(
            lax.slice_in_dim(block, block.shape[dim] - width, None, axis=dim), axis, forward
        )
        high = lax.ppermute(lax.slice_in_dim(block, 0, width, axis=dim), axis, backward)
        block = jnp.concatenate([low, block, high], axis=dim)
    return block


def gelu_tanh(value):
    return jax.nn.gelu(value, approximate=True)


def point_flat(spread, weight, rows, cols):
    chans = weight.shape[0]
    flat = spread.astype(jnp.bfloat16).reshape(rows * cols, chans)
    mixed = jnp.dot(flat, weight, preferred_element_type=jnp.float32)
    return gelu_tanh(mixed).reshape(rows, cols * weight.shape[1])


def down_level(field, taps, weight, split_rows, split_cols):
    chans = taps.shape[1]
    rows = field.shape[0]
    cols = field.shape[1] // chans
    half_rows = rows // 2
    half_cols = cols // 2
    if split_rows:
        upper = shifted(field[-1:], "gx", 1)
    else:
        upper = jnp.zeros((1, cols * chans), jnp.bfloat16)
    extended = jnp.concatenate([upper, field], axis=0)
    if split_cols:
        leftside = shifted(extended[:, -chans:], "gy", 1)
    else:
        leftside = jnp.zeros((rows + 1, chans), jnp.bfloat16)
    tiled = jnp.tile(taps, (1, half_cols))
    total = jnp.zeros((half_rows, half_cols * chans), jnp.float32)
    for first in range(3):
        slab = extended[first : first + rows : 2]
        left_slab = leftside[first : first + rows : 2]
        pairs = slab.reshape(half_rows, half_cols, 2 * chans)
        even_cells = pairs[:, :, :chans].reshape(half_rows, half_cols * chans)
        odd_cells = pairs[:, :, chans:].reshape(half_rows, half_cols * chans)
        before = jnp.concatenate([left_slab, odd_cells[:, :-chans]], axis=1)
        for second, piece in enumerate((before, even_cells, odd_cells)):
            total = total + piece.astype(jnp.float32) * tiled[3 * first + second]
    return point_flat(total, weight, half_rows, half_cols).astype(jnp.bfloat16)


def strided_flat(ext, taps, weight):
    chans = taps.shape[1]
    rows = (ext.shape[0] - 1) // 2
    cols = (ext.shape[1] // chans - 1) // 2
    tiled = jnp.tile(taps, (1, cols))
    total = jnp.zeros((rows, cols * chans), jnp.float32)
    for first in range(3):
        slab = ext[first : first + 2 * rows : 2]
        head = slab[:, : 2 * cols * chans].reshape(rows, cols, 2 * chans)
        tail = slab[:, chans:].reshape(rows, cols, 2 * chans)
        pieces = (head[:, :, :chans], head[:, :, chans:], tail[:, :, chans:])
        for second, piece in enumerate(pieces):
            piece = piece.reshape(rows, cols * chans)
            total = total + piece.astype(jnp.float32) * tiled[3 * first + second]
    return point_flat(total, weight, rows, cols).astype(jnp.bfloat16)


def local(field, dw0, pw0, dw1, pw1, dw2, pw2, dw3, pw3, dw4, pw4, dwc, pwc):
    chans = dw0.shape[1]
    rows = field.shape[0]
    cols = field.shape[1] // chans
    depth = 4
    margin = 2**depth - 1
    upper = shifted(field[-margin - 2 :], "gx", 1)
    lower = shifted(field[:2], "gx", -1)
    stacked = jnp.concatenate([upper, field, lower], axis=0)
    leftside = shifted(stacked[:, -(margin + 2) * chans :], "gy", 1)
    rightside = shifted(stacked[:, : 2 * chans], "gy", -1)
    flat_pad = jnp.concatenate([leftside, stacked, rightside], axis=1)
    ext_rows = rows + margin
    ext_cols = cols + margin
    tiled = jnp.tile(dw0, (1, ext_cols))
    total = jnp.zeros((ext_rows, ext_cols * chans), jnp.float32)
    for first in range(3):
        for second in range(3):
            piece = flat_pad[
                2 * first : 2 * first + ext_rows,
                2 * second * chans : 2 * second * chans + ext_cols * chans,
            ]
            total = total + piece.astype(jnp.float32) * tiled[3 * first + second]
    centre = flat_pad[2 : 2 + ext_rows, 2 * chans : 2 * chans + ext_cols * chans]
    hidden = (centre.astype(jnp.float32) + point_flat(total, pw0, ext_rows, ext_cols)).astype(
        jnp.bfloat16
    )
    row_ok = (lax.axis_index("gx") > 0) | (lax.broadcasted_iota(jnp.int32, hidden.shape, 0) >= margin)
    col_ok = (lax.axis_index("gy") > 0) | (
        lax.broadcasted_iota(jnp.int32, hidden.shape, 1) >= margin * chans
    )
    hidden = jnp.where(row_ok & col_ok, hidden, jnp.zeros_like(hidden))
    fine = hidden[margin:, margin * chans :]
    for taps, weight in ((dw1, pw1), (dw2, pw2), (dw3, pw3), (dw4, pw4)):
        hidden = strided_flat(hidden, taps, weight)
    coarse_chans = dwc.shape[2]
    halo = 2 ** (LC - 1) - 1
    grid4 = hidden.reshape(hidden.shape[0], -1, coarse_chans)
    upper = shifted(grid4[-1:], "gx", 1)
    extended = jnp.concatenate([upper, grid4], axis=0)
    leftside = shifted(extended[:, -halo:], "gy", 1)
    extended = jnp.concatenate([leftside, extended], axis=1)
    hidden = strided_cells(extended, dwc[0], pwc[0])
    hidden = doubling_gather(hidden, "gx", 0)
    for level in range(1, LC - 1):
        hidden = strided_cells(pad_top(hidden), dwc[level], pwc[level])
    hidden = doubling_gather(hidden, "gy", 1)
    hidden = strided_cells(pad_left(pad_top(hidden)), dwc[LC - 1], pwc[LC - 1])
    return (fine, hidden.reshape(hidden.shape[0], -1))


def doubling_gather(block, axis, dim):
    count = lax.axis_size(axis)
    index = lax.axis_index(axis)
    span = 1
    while span < count:
        pairs = [(source, source ^ span) for source in range(count)]
        other = lax.ppermute(block, axis, pairs)
        later = (index // span) % 2 == 1
        block = jnp.where(
            later,
            jnp.concatenate([other, block], axis=dim),
            jnp.concatenate([block, other], axis=dim),
        )
        span *= 2
    return block


def pad_top(cells):
    return jnp.concatenate([jnp.zeros_like(cells[:1]), cells], axis=0)


def pad_left(cells):
    return jnp.concatenate([jnp.zeros_like(cells[:, :1]), cells], axis=1)


def strided_cells(padded, taps, weight):
    rows = (padded.shape[0] - 1) // 2
    cols = (padded.shape[1] - 1) // 2
    total = jnp.zeros((rows, cols, padded.shape[2]), jnp.float32)
    for first in range(3):
        for second in range(3):
            piece = padded[first : first + 2 * rows : 2, second : second + 2 * cols : 2]
            total = total + piece.astype(jnp.float32) * taps[3 * first + second]
    flat = total.astype(jnp.bfloat16).reshape(rows * cols, -1)
    mixed = jnp.dot(flat, weight, preferred_element_type=jnp.float32)
    return gelu_tanh(mixed).astype(jnp.bfloat16).reshape(rows, cols, weight.shape[1])


def solution(mesh):
    placed = (P("gx", "gy"), P(), P(), P(), P(), P(), P(), P(), P(), P(), P(), P(), P())
    return jax.shard_map(
        local, mesh=mesh, in_specs=placed, out_specs=(P("gx", "gy"), P()), check_vma=False
    )
```

```python
import jax
import jax.numpy as jnp
from jax import lax
from jax.sharding import PartitionSpec as P

LC = 4
ROW_AXES = ("zh", "zl", "core")
COL_AXES = ("x", "y")


def shifted(value, axis, steps):
    count = axis_count(axis)
    leading, last = (max(0, -steps), min(count, count - steps))
    return lax.ppermute(value, axis, [(source, source + steps) for source in range(leading, last)])


def axis_count(axes):
    count = 1
    for axis in axes:
        count *= lax.axis_size(axis)
    return count


def padded_2(block, sides, width):
    for axis, dim in sides:
        count = axis_count(axis)
        forward = [(i, i + 1) for i in range(count - 1)]
        backward = [(target, source) for source, target in forward]
        low = lax.ppermute(
            lax.slice_in_dim(block, block.shape[dim] - width, None, axis=dim), axis, forward
        )
        high = lax.ppermute(lax.slice_in_dim(block, 0, width, axis=dim), axis, backward)
        block = jnp.concatenate([low, block, high], axis=dim)
    return block


def gelu_tanh(value):
    return jax.nn.gelu(value, approximate=True)


def point_flat(spread, weight, rows, cols):
    chans = weight.shape[0]
    flat = spread.astype(jnp.bfloat16).reshape(rows * cols, chans)
    mixed = jnp.dot(flat, weight, preferred_element_type=jnp.float32)
    return gelu_tanh(mixed).reshape(rows, cols * weight.shape[1])


def down_level(field, taps, weight, split_rows, split_cols):
    chans = taps.shape[1]
    rows = field.shape[0]
    cols = field.shape[1] // chans
    half_rows = rows // 2
    half_cols = cols // 2
    if split_rows:
        upper = shifted(field[-1:], ROW_AXES, 1)
    else:
        upper = jnp.zeros((1, cols * chans), jnp.bfloat16)
    extended = jnp.concatenate([upper, field], axis=0)
    if split_cols:
        leftside = shifted(extended[:, -chans:], COL_AXES, 1)
    else:
        leftside = jnp.zeros((rows + 1, chans), jnp.bfloat16)
    tiled = jnp.tile(taps, (1, half_cols))
    total = jnp.zeros((half_rows, half_cols * chans), jnp.float32)
    for first in range(3):
        slab = extended[first : first + rows : 2]
        left_slab = leftside[first : first + rows : 2]
        pairs = slab.reshape(half_rows, half_cols, 2 * chans)
        even_cells = pairs[:, :, :chans].reshape(half_rows, half_cols * chans)
        odd_cells = pairs[:, :, chans:].reshape(half_rows, half_cols * chans)
        before = jnp.concatenate([left_slab, odd_cells[:, :-chans]], axis=1)
        for second, piece in enumerate((before, even_cells, odd_cells)):
            total = total + piece.astype(jnp.float32) * tiled[3 * first + second]
    return point_flat(total, weight, half_rows, half_cols).astype(jnp.bfloat16)


def strided_flat(ext, taps, weight):
    chans = taps.shape[1]
    rows = (ext.shape[0] - 1) // 2
    cols = (ext.shape[1] // chans - 1) // 2
    tiled = jnp.tile(taps, (1, cols))
    total = jnp.zeros((rows, cols * chans), jnp.float32)
    for first in range(3):
        slab = ext[first : first + 2 * rows : 2]
        head = slab[:, : 2 * cols * chans].reshape(rows, cols, 2 * chans)
        tail = slab[:, chans:].reshape(rows, cols, 2 * chans)
        pieces = (head[:, :, :chans], head[:, :, chans:], tail[:, :, chans:])
        for second, piece in enumerate(pieces):
            piece = piece.reshape(rows, cols * chans)
            total = total + piece.astype(jnp.float32) * tiled[3 * first + second]
    return point_flat(total, weight, rows, cols).astype(jnp.bfloat16)


def local(field, dw0, pw0, dw1, pw1, dw2, pw2, dw3, pw3, dw4, pw4, dwc, pwc):
    chans = dw0.shape[1]
    rows = field.shape[0]
    cols = field.shape[1] // chans
    depth = 4
    margin = 2**depth - 1
    upper = shifted(field[-margin - 2 :], ROW_AXES, 1)
    lower = shifted(field[:2], ROW_AXES, -1)
    stacked = jnp.concatenate([upper, field, lower], axis=0)
    leftside = shifted(stacked[:, -(margin + 2) * chans :], COL_AXES, 1)
    rightside = shifted(stacked[:, : 2 * chans], COL_AXES, -1)
    flat_pad = jnp.concatenate([leftside, stacked, rightside], axis=1)
    ext_rows = rows + margin
    ext_cols = cols + margin
    tiled = jnp.tile(dw0, (1, ext_cols))
    total = jnp.zeros((ext_rows, ext_cols * chans), jnp.float32)
    for first in range(3):
        for second in range(3):
            piece = flat_pad[
                2 * first : 2 * first + ext_rows,
                2 * second * chans : 2 * second * chans + ext_cols * chans,
            ]
            total = total + piece.astype(jnp.float32) * tiled[3 * first + second]
    centre = flat_pad[2 : 2 + ext_rows, 2 * chans : 2 * chans + ext_cols * chans]
    hidden = (centre.astype(jnp.float32) + point_flat(total, pw0, ext_rows, ext_cols)).astype(
        jnp.bfloat16
    )
    row_ok = (lax.axis_index(ROW_AXES) > 0) | (lax.broadcasted_iota(jnp.int32, hidden.shape, 0) >= margin)
    col_ok = (lax.axis_index(COL_AXES) > 0) | (
        lax.broadcasted_iota(jnp.int32, hidden.shape, 1) >= margin * chans
    )
    hidden = jnp.where(row_ok & col_ok, hidden, jnp.zeros_like(hidden))
    fine = hidden[margin:, margin * chans :]
    for taps, weight in ((dw1, pw1), (dw2, pw2), (dw3, pw3), (dw4, pw4)):
        hidden = strided_flat(hidden, taps, weight)
    coarse_chans = dwc.shape[2]
    halo = 2 ** (LC - 1) - 1
    grid4 = hidden.reshape(hidden.shape[0], -1, coarse_chans)
    upper = shifted(grid4[-1:], ROW_AXES, 1)
    extended = jnp.concatenate([upper, grid4], axis=0)
    leftside = shifted(extended[:, -halo:], COL_AXES, 1)
    extended = jnp.concatenate([leftside, extended], axis=1)
    hidden = strided_cells(extended, dwc[0], pwc[0])
    for axis in reversed(ROW_AXES):
        hidden = lax.all_gather(hidden, axis, axis=0, tiled=True)
    for level in range(1, LC - 1):
        hidden = strided_cells(pad_top(hidden), dwc[level], pwc[level])
    for axis in reversed(COL_AXES):
        hidden = lax.all_gather(hidden, axis, axis=1, tiled=True)
    hidden = strided_cells(pad_left(pad_top(hidden)), dwc[LC - 1], pwc[LC - 1])
    return (fine, hidden.reshape(hidden.shape[0], -1))


def pad_top(cells):
    return jnp.concatenate([jnp.zeros_like(cells[:1]), cells], axis=0)


def pad_left(cells):
    return jnp.concatenate([jnp.zeros_like(cells[:, :1]), cells], axis=1)


def strided_cells(padded, taps, weight):
    rows = (padded.shape[0] - 1) // 2
    cols = (padded.shape[1] - 1) // 2
    total = jnp.zeros((rows, cols, padded.shape[2]), jnp.float32)
    for first in range(3):
        for second in range(3):
            piece = padded[first : first + 2 * rows : 2, second : second + 2 * cols : 2]
            total = total + piece.astype(jnp.float32) * taps[3 * first + second]
    flat = total.astype(jnp.bfloat16).reshape(rows * cols, -1)
    mixed = jnp.dot(flat, weight, preferred_element_type=jnp.float32)
    return gelu_tanh(mixed).astype(jnp.bfloat16).reshape(rows, cols, weight.shape[1])


def solution(mesh):
    rows, cols = mesh.devices.shape
    split = mesh.devices.reshape(rows // 8, 4, 2, cols // 4, 4)
    fine_mesh = jax.sharding.Mesh(split, ROW_AXES + COL_AXES)
    grid = P(ROW_AXES, COL_AXES)
    placed = (grid,) + (P(),) * 12
    return jax.shard_map(
        local, mesh=fine_mesh, in_specs=placed, out_specs=(grid, P()), check_vma=False
    )
```

```python
import jax
import jax.numpy as jnp
from jax import lax
from jax.sharding import PartitionSpec as P

LC = 4


def shifted(value, axis, steps):
    count = lax.axis_size(axis)
    leading, last = (max(0, -steps), min(count, count - steps))
    return lax.ppermute(value, axis, [(source, source + steps) for source in range(leading, last)])


def padded_2(block, sides, width):
    for axis, dim in sides:
        count = lax.axis_size(axis)
        forward = [(i, i + 1) for i in range(count - 1)]
        backward = [(target, source) for source, target in forward]
        low = lax.ppermute(
            lax.slice_in_dim(block, block.shape[dim] - width, None, axis=dim), axis, forward
        )
        high = lax.ppermute(lax.slice_in_dim(block, 0, width, axis=dim), axis, backward)
        block = jnp.concatenate([low, block, high], axis=dim)
    return block


def gelu_tanh(value):
    return jax.nn.gelu(value, approximate=True)


def point_flat(spread, weight, rows, cols):
    chans = weight.shape[0]
    flat = spread.astype(jnp.bfloat16).reshape(rows * cols, chans)
    mixed = jnp.dot(flat, weight, preferred_element_type=jnp.float32)
    return gelu_tanh(mixed).reshape(rows, cols * weight.shape[1])


def down_level(field, taps, weight, split_rows, split_cols):
    chans = taps.shape[1]
    rows = field.shape[0]
    cols = field.shape[1] // chans
    half_rows = rows // 2
    half_cols = cols // 2
    if split_rows:
        upper = shifted(field[-1:], "gx", 1)
    else:
        upper = jnp.zeros((1, cols * chans), jnp.bfloat16)
    extended = jnp.concatenate([upper, field], axis=0)
    if split_cols:
        leftside = shifted(extended[:, -chans:], "gy", 1)
    else:
        leftside = jnp.zeros((rows + 1, chans), jnp.bfloat16)
    tiled = jnp.tile(taps, (1, half_cols))
    total = jnp.zeros((half_rows, half_cols * chans), jnp.float32)
    for first in range(3):
        slab = extended[first : first + rows : 2]
        left_slab = leftside[first : first + rows : 2]
        pairs = slab.reshape(half_rows, half_cols, 2 * chans)
        even_cells = pairs[:, :, :chans].reshape(half_rows, half_cols * chans)
        odd_cells = pairs[:, :, chans:].reshape(half_rows, half_cols * chans)
        before = jnp.concatenate([left_slab, odd_cells[:, :-chans]], axis=1)
        for second, piece in enumerate((before, even_cells, odd_cells)):
            total = total + piece.astype(jnp.float32) * tiled[3 * first + second]
    return point_flat(total, weight, half_rows, half_cols).astype(jnp.bfloat16)


def strided_flat(ext, taps, weight):
    chans = taps.shape[1]
    rows = (ext.shape[0] - 1) // 2
    cols = (ext.shape[1] // chans - 1) // 2
    tiled = jnp.tile(taps, (1, cols))
    total = jnp.zeros((rows, cols * chans), jnp.float32)
    for first in range(3):
        slab = ext[first : first + 2 * rows : 2]
        head = slab[:, : 2 * cols * chans].reshape(rows, cols, 2 * chans)
        tail = slab[:, chans:].reshape(rows, cols, 2 * chans)
        pieces = (head[:, :, :chans], head[:, :, chans:], tail[:, :, chans:])
        for second, piece in enumerate(pieces):
            piece = piece.reshape(rows, cols * chans)
            total = total + piece.astype(jnp.float32) * tiled[3 * first + second]
    return point_flat(total, weight, rows, cols).astype(jnp.bfloat16)


def local(field, dw0, pw0, dw1, pw1, dw2, pw2, dw3, pw3, dw4, pw4, dwc, pwc):
    chans = dw0.shape[1]
    rows = field.shape[0]
    cols = field.shape[1] // chans
    depth = 4
    margin = 2**depth - 1
    upper = shifted(field[-margin - 2 :], "gx", 1)
    lower = shifted(field[:2], "gx", -1)
    stacked = jnp.concatenate([upper, field, lower], axis=0)
    leftside = shifted(stacked[:, -(margin + 2) * chans :], "gy", 1)
    rightside = shifted(stacked[:, : 2 * chans], "gy", -1)
    flat_pad = jnp.concatenate([leftside, stacked, rightside], axis=1)
    ext_rows = rows + margin
    ext_cols = cols + margin
    tiled = jnp.tile(dw0, (1, ext_cols))
    total = jnp.zeros((ext_rows, ext_cols * chans), jnp.float32)
    for first in range(3):
        for second in range(3):
            piece = flat_pad[
                2 * first : 2 * first + ext_rows,
                2 * second * chans : 2 * second * chans + ext_cols * chans,
            ]
            total = total + piece.astype(jnp.float32) * tiled[3 * first + second]
    centre = flat_pad[2 : 2 + ext_rows, 2 * chans : 2 * chans + ext_cols * chans]
    flat = total.astype(jnp.bfloat16).reshape(ext_rows * ext_cols, chans)
    mixed = gelu_tanh(jnp.dot(flat, pw0, preferred_element_type=jnp.float32))
    centre = centre.reshape(ext_rows * ext_cols, chans).astype(jnp.float32)
    hidden = (centre + mixed).astype(jnp.bfloat16).reshape(ext_rows, ext_cols, chans)
    row_ok = (lax.axis_index("gx") > 0) | (lax.broadcasted_iota(jnp.int32, hidden.shape, 0) >= margin)
    col_ok = (lax.axis_index("gy") > 0) | (lax.broadcasted_iota(jnp.int32, hidden.shape, 1) >= margin)
    hidden = jnp.where(row_ok & col_ok, hidden, jnp.zeros_like(hidden))
    fine = hidden[margin:, margin:].reshape(rows, cols * chans)
    for taps, weight in ((dw1, pw1), (dw2, pw2), (dw3, pw3), (dw4, pw4)):
        hidden = strided_cells(hidden, taps, weight)
    coarse_chans = dwc.shape[2]
    halo = 2 ** (LC - 1) - 1
    grid4 = hidden
    upper = shifted(grid4[-1:], "gx", 1)
    extended = jnp.concatenate([upper, grid4], axis=0)
    leftside = shifted(extended[:, -halo:], "gy", 1)
    extended = jnp.concatenate([leftside, extended], axis=1)
    hidden = strided_cells(extended, dwc[0], pwc[0])
    hidden = lax.all_gather(hidden, "gx", axis=0, tiled=True)
    for level in range(1, LC - 1):
        hidden = strided_cells(pad_top(hidden), dwc[level], pwc[level])
    hidden = lax.all_gather(hidden, "gy", axis=1, tiled=True)
    hidden = strided_cells(pad_left(pad_top(hidden)), dwc[LC - 1], pwc[LC - 1])
    return (fine, hidden.reshape(hidden.shape[0], -1))


def pad_top(cells):
    return jnp.concatenate([jnp.zeros_like(cells[:1]), cells], axis=0)


def pad_left(cells):
    return jnp.concatenate([jnp.zeros_like(cells[:, :1]), cells], axis=1)


def strided_cells(padded, taps, weight):
    rows = (padded.shape[0] - 1) // 2
    cols = (padded.shape[1] - 1) // 2
    total = jnp.zeros((rows, cols, padded.shape[2]), jnp.float32)
    for first in range(3):
        for second in range(3):
            piece = padded[first : first + 2 * rows : 2, second : second + 2 * cols : 2]
            total = total + piece.astype(jnp.float32) * taps[3 * first + second]
    flat = total.astype(jnp.bfloat16).reshape(rows * cols, -1)
    mixed = jnp.dot(flat, weight, preferred_element_type=jnp.float32)
    return gelu_tanh(mixed).astype(jnp.bfloat16).reshape(rows, cols, weight.shape[1])


def solution(mesh):
    placed = (P("gx", "gy"), P(), P(), P(), P(), P(), P(), P(), P(), P(), P(), P(), P())
    return jax.shard_map(
        local, mesh=mesh, in_specs=placed, out_specs=(P("gx", "gy"), P()), check_vma=False
    )
```

```python
import jax
import jax.numpy as jnp
from jax import lax
from jax.sharding import PartitionSpec as P

LC = 4


def shifted(value, axis, steps):
    count = lax.axis_size(axis)
    leading, last = (max(0, -steps), min(count, count - steps))
    return lax.ppermute(value, axis, [(source, source + steps) for source in range(leading, last)])


def padded_2(block, sides, width):
    for axis, dim in sides:
        count = lax.axis_size(axis)
        forward = [(i, i + 1) for i in range(count - 1)]
        backward = [(target, source) for source, target in forward]
        low = lax.ppermute(
            lax.slice_in_dim(block, block.shape[dim] - width, None, axis=dim), axis, forward
        )
        high = lax.ppermute(lax.slice_in_dim(block, 0, width, axis=dim), axis, backward)
        block = jnp.concatenate([low, block, high], axis=dim)
    return block


def moved(value, down, right):
    rows = lax.axis_size("gx")
    cols = lax.axis_size("gy")
    pairs = []
    for row in range(rows):
        for col in range(cols):
            if 0 <= row + down < rows and 0 <= col + right < cols:
                pairs.append((row * cols + col, (row + down) * cols + col + right))
    return lax.ppermute(value, ("gx", "gy"), pairs)


def gelu_tanh(value):
    return jax.nn.gelu(value, approximate=True)


def point_flat(spread, weight, rows, cols):
    chans = weight.shape[0]
    flat = spread.astype(jnp.bfloat16).reshape(rows * cols, chans)
    mixed = jnp.dot(flat, weight, preferred_element_type=jnp.float32)
    return gelu_tanh(mixed).reshape(rows, cols * weight.shape[1])


def down_level(field, taps, weight, split_rows, split_cols):
    chans = taps.shape[1]
    rows = field.shape[0]
    cols = field.shape[1] // chans
    half_rows = rows // 2
    half_cols = cols // 2
    if split_rows:
        upper = shifted(field[-1:], "gx", 1)
    else:
        upper = jnp.zeros((1, cols * chans), jnp.bfloat16)
    extended = jnp.concatenate([upper, field], axis=0)
    if split_cols:
        leftside = shifted(extended[:, -chans:], "gy", 1)
    else:
        leftside = jnp.zeros((rows + 1, chans), jnp.bfloat16)
    tiled = jnp.tile(taps, (1, half_cols))
    total = jnp.zeros((half_rows, half_cols * chans), jnp.float32)
    for first in range(3):
        slab = extended[first : first + rows : 2]
        left_slab = leftside[first : first + rows : 2]
        pairs = slab.reshape(half_rows, half_cols, 2 * chans)
        even_cells = pairs[:, :, :chans].reshape(half_rows, half_cols * chans)
        odd_cells = pairs[:, :, chans:].reshape(half_rows, half_cols * chans)
        before = jnp.concatenate([left_slab, odd_cells[:, :-chans]], axis=1)
        for second, piece in enumerate((before, even_cells, odd_cells)):
            total = total + piece.astype(jnp.float32) * tiled[3 * first + second]
    return point_flat(total, weight, half_rows, half_cols).astype(jnp.bfloat16)


def strided_flat(ext, taps, weight):
    chans = taps.shape[1]
    rows = (ext.shape[0] - 1) // 2
    cols = (ext.shape[1] // chans - 1) // 2
    tiled = jnp.tile(taps, (1, cols))
    total = jnp.zeros((rows, cols * chans), jnp.float32)
    for first in range(3):
        slab = ext[first : first + 2 * rows : 2]
        head = slab[:, : 2 * cols * chans].reshape(rows, cols, 2 * chans)
        tail = slab[:, chans:].reshape(rows, cols, 2 * chans)
        pieces = (head[:, :, :chans], head[:, :, chans:], tail[:, :, chans:])
        for second, piece in enumerate(pieces):
            piece = piece.reshape(rows, cols * chans)
            total = total + piece.astype(jnp.float32) * tiled[3 * first + second]
    return point_flat(total, weight, rows, cols).astype(jnp.bfloat16)


def local(field, dw0, pw0, dw1, pw1, dw2, pw2, dw3, pw3, dw4, pw4, dwc, pwc):
    chans = dw0.shape[1]
    rows = field.shape[0]
    cols = field.shape[1] // chans
    depth = 4
    margin = 2**depth - 1
    top = margin + 2
    edges = {}
    for down, row_part in ((1, field[-top:]), (0, field), (-1, field[:2])):
        for right, width in ((1, top), (0, None), (-1, 2)):
            if width is None:
                part = row_part
            elif right == 1:
                part = row_part[:, -width * chans :]
            else:
                part = row_part[:, : width * chans]
            edges[down, right] = part if down == right == 0 else moved(part, down, right)
    flat_pad = jnp.concatenate(
        [
            jnp.concatenate([edges[down, right] for right in (1, 0, -1)], axis=1)
            for down in (1, 0, -1)
        ],
        axis=0,
    )
    ext_rows = rows + margin
    ext_cols = cols + margin
    tiled = jnp.tile(dw0, (1, ext_cols))
    total = jnp.zeros((ext_rows, ext_cols * chans), jnp.float32)
    for first in range(3):
        for second in range(3):
            piece = flat_pad[
                2 * first : 2 * first + ext_rows,
                2 * second * chans : 2 * second * chans + ext_cols * chans,
            ]
            total = total + piece.astype(jnp.float32) * tiled[3 * first + second]
    centre = flat_pad[2 : 2 + ext_rows, 2 * chans : 2 * chans + ext_cols * chans]
    hidden = (centre.astype(jnp.float32) + point_flat(total, pw0, ext_rows, ext_cols)).astype(
        jnp.bfloat16
    )
    row_ok = (lax.axis_index("gx") > 0) | (lax.broadcasted_iota(jnp.int32, hidden.shape, 0) >= margin)
    col_ok = (lax.axis_index("gy") > 0) | (
        lax.broadcasted_iota(jnp.int32, hidden.shape, 1) >= margin * chans
    )
    hidden = jnp.where(row_ok & col_ok, hidden, jnp.zeros_like(hidden))
    fine = hidden[margin:, margin * chans :]
    for taps, weight in ((dw1, pw1), (dw2, pw2), (dw3, pw3), (dw4, pw4)):
        hidden = strided_flat(hidden, taps, weight)
    coarse_chans = dwc.shape[2]
    halo = 2 ** (LC - 1) - 1
    grid4 = hidden.reshape(hidden.shape[0], -1, coarse_chans)
    upper = shifted(grid4[-1:], "gx", 1)
    extended = jnp.concatenate([upper, grid4], axis=0)
    leftside = shifted(extended[:, -halo:], "gy", 1)
    extended = jnp.concatenate([leftside, extended], axis=1)
    hidden = strided_cells(extended, dwc[0], pwc[0])
    hidden = lax.all_gather(hidden, "gx", axis=0, tiled=True)
    for level in range(1, LC - 1):
        hidden = strided_cells(pad_top(hidden), dwc[level], pwc[level])
    hidden = lax.all_gather(hidden, "gy", axis=1, tiled=True)
    hidden = strided_cells(pad_left(pad_top(hidden)), dwc[LC - 1], pwc[LC - 1])
    return (fine, hidden.reshape(hidden.shape[0], -1))


def pad_top(cells):
    return jnp.concatenate([jnp.zeros_like(cells[:1]), cells], axis=0)


def pad_left(cells):
    return jnp.concatenate([jnp.zeros_like(cells[:, :1]), cells], axis=1)


def strided_cells(padded, taps, weight):
    rows = (padded.shape[0] - 1) // 2
    cols = (padded.shape[1] - 1) // 2
    total = jnp.zeros((rows, cols, padded.shape[2]), jnp.float32)
    for first in range(3):
        for second in range(3):
            piece = padded[first : first + 2 * rows : 2, second : second + 2 * cols : 2]
            total = total + piece.astype(jnp.float32) * taps[3 * first + second]
    flat = total.astype(jnp.bfloat16).reshape(rows * cols, -1)
    mixed = jnp.dot(flat, weight, preferred_element_type=jnp.float32)
    return gelu_tanh(mixed).astype(jnp.bfloat16).reshape(rows, cols, weight.shape[1])


def solution(mesh):
    placed = (P("gx", "gy"), P(), P(), P(), P(), P(), P(), P(), P(), P(), P(), P(), P())
    return jax.shard_map(
        local, mesh=mesh, in_specs=placed, out_specs=(P("gx", "gy"), P()), check_vma=False
    )
```

```python
import functools

import jax
import jax.numpy as jnp
from jax import lax
from jax.experimental import pallas as pl
from jax.experimental.pallas import tpu as pltpu
from jax.sharding import PartitionSpec as P

LC = 4


def shifted(value, axis, steps):
    count = lax.axis_size(axis)
    leading, last = (max(0, -steps), min(count, count - steps))
    return lax.ppermute(value, axis, [(source, source + steps) for source in range(leading, last)])


def padded_2(block, sides, width):
    for axis, dim in sides:
        count = lax.axis_size(axis)
        forward = [(i, i + 1) for i in range(count - 1)]
        backward = [(target, source) for source, target in forward]
        low = lax.ppermute(
            lax.slice_in_dim(block, block.shape[dim] - width, None, axis=dim), axis, forward
        )
        high = lax.ppermute(lax.slice_in_dim(block, 0, width, axis=dim), axis, backward)
        block = jnp.concatenate([low, block, high], axis=dim)
    return block


def gelu_tanh(value):
    return jax.nn.gelu(value, approximate=True)


def point_flat(spread, weight, rows, cols):
    chans = weight.shape[0]
    flat = spread.astype(jnp.bfloat16).reshape(rows * cols, chans)
    mixed = jnp.dot(flat, weight, preferred_element_type=jnp.float32)
    return gelu_tanh(mixed).reshape(rows, cols * weight.shape[1])


def down_level(field, taps, weight, split_rows, split_cols):
    chans = taps.shape[1]
    rows = field.shape[0]
    cols = field.shape[1] // chans
    half_rows = rows // 2
    half_cols = cols // 2
    if split_rows:
        upper = shifted(field[-1:], "gx", 1)
    else:
        upper = jnp.zeros((1, cols * chans), jnp.bfloat16)
    extended = jnp.concatenate([upper, field], axis=0)
    if split_cols:
        leftside = shifted(extended[:, -chans:], "gy", 1)
    else:
        leftside = jnp.zeros((rows + 1, chans), jnp.bfloat16)
    tiled = jnp.tile(taps, (1, half_cols))
    total = jnp.zeros((half_rows, half_cols * chans), jnp.float32)
    for first in range(3):
        slab = extended[first : first + rows : 2]
        left_slab = leftside[first : first + rows : 2]
        pairs = slab.reshape(half_rows, half_cols, 2 * chans)
        even_cells = pairs[:, :, :chans].reshape(half_rows, half_cols * chans)
        odd_cells = pairs[:, :, chans:].reshape(half_rows, half_cols * chans)
        before = jnp.concatenate([left_slab, odd_cells[:, :-chans]], axis=1)
        for second, piece in enumerate((before, even_cells, odd_cells)):
            total = total + piece.astype(jnp.float32) * tiled[3 * first + second]
    return point_flat(total, weight, half_rows, half_cols).astype(jnp.bfloat16)


def strided_flat(ext, taps, weight):
    chans = taps.shape[1]
    rows = (ext.shape[0] - 1) // 2
    cols = (ext.shape[1] // chans - 1) // 2
    tiled = jnp.tile(taps, (1, cols))
    total = jnp.zeros((rows, cols * chans), jnp.float32)
    for first in range(3):
        slab = ext[first : first + 2 * rows : 2]
        head = slab[:, : 2 * cols * chans].reshape(rows, cols, 2 * chans)
        tail = slab[:, chans:].reshape(rows, cols, 2 * chans)
        pieces = (head[:, :, :chans], head[:, :, chans:], tail[:, :, chans:])
        for second, piece in enumerate(pieces):
            piece = piece.reshape(rows, cols * chans)
            total = total + piece.astype(jnp.float32) * tiled[3 * first + second]
    return point_flat(total, weight, rows, cols).astype(jnp.bfloat16)


def pair_kernel(even_ref, odd_ref, near_ref, far_ref, w_ref, o_ref, *, rows, chans, chunk, width):
    lanes = even_ref.shape[1]
    total = None
    for first in range(3):
        if first == 1:
            slab = odd_ref[...]
        else:
            slab = even_ref[pl.ds(first // 2, rows), :]
        ahead = pltpu.roll(slab, lanes - 2 * chans, 1)
        term = slab * near_ref[first : first + 1, :] + ahead * far_ref[first : first + 1, :]
        total = term if total is None else total + term
    weight = w_ref[...]
    for index in range(lanes // chunk):
        part = jnp.dot(
            total[:, index * chunk : (index + 1) * chunk],
            weight,
            preferred_element_type=jnp.float32,
        )
        o_ref[:, index * width : (index + 1) * width] = gelu_tanh(part).astype(o_ref.dtype)


def strided_kernel(ext, taps, weight):
    chans = taps.shape[1]
    outs = weight.shape[1]
    rows = (ext.shape[0] - 1) // 2
    cols = (ext.shape[1] // chans - 1) // 2
    pairs = cols + 1
    if pairs * 2 * chans % 128:
        pairs += 1
    padded_rows = -(-rows // 8) * 8
    lanes = pairs * 2 * chans
    source = jnp.pad(
        ext.astype(jnp.float32),
        ((0, 2 * padded_rows + 1 - ext.shape[0]), (0, lanes - ext.shape[1])),
    )
    zero = jnp.zeros_like(taps[0])
    near = jnp.stack(
        [jnp.tile(jnp.concatenate([taps[3 * a], taps[3 * a + 1]]), pairs) for a in range(3)]
    )
    far = jnp.stack([jnp.tile(jnp.concatenate([taps[3 * a + 2], zero]), pairs) for a in range(3)])
    chunk = max(128, 2 * chans)
    group = chunk // (2 * chans)
    doubled = jnp.concatenate([weight, weight], axis=0).astype(jnp.float32)
    block = jnp.kron(jnp.eye(group, dtype=jnp.float32), doubled)
    width = group * outs
    body = functools.partial(pair_kernel, rows=padded_rows, chans=chans, chunk=chunk, width=width)
    result = pl.pallas_call(
        body,
        out_shape=jax.ShapeDtypeStruct((padded_rows, pairs * outs), jnp.bfloat16),
    )(source[0::2], source[1::2], near, far, block)
    return result[:rows, : cols * outs]


def local(field, dw0, pw0, dw1, pw1, dw2, pw2, dw3, pw3, dw4, pw4, dwc, pwc):
    chans = dw0.shape[1]
    rows = field.shape[0]
    cols = field.shape[1] // chans
    depth = 4
    margin = 2**depth - 1
    upper = shifted(field[-margin - 2 :], "gx", 1)
    lower = shifted(field[:2], "gx", -1)
    stacked = jnp.concatenate([upper, field, lower], axis=0)
    leftside = shifted(stacked[:, -(margin + 2) * chans :], "gy", 1)
    rightside = shifted(stacked[:, : 2 * chans], "gy", -1)
    flat_pad = jnp.concatenate([leftside, stacked, rightside], axis=1)
    ext_rows = rows + margin
    ext_cols = cols + margin
    tiled = jnp.tile(dw0, (1, ext_cols))
    total = jnp.zeros((ext_rows, ext_cols * chans), jnp.float32)
    for first in range(3):
        for second in range(3):
            piece = flat_pad[
                2 * first : 2 * first + ext_rows,
                2 * second * chans : 2 * second * chans + ext_cols * chans,
            ]
            total = total + piece.astype(jnp.float32) * tiled[3 * first + second]
    centre = flat_pad[2 : 2 + ext_rows, 2 * chans : 2 * chans + ext_cols * chans]
    hidden = (centre.astype(jnp.float32) + point_flat(total, pw0, ext_rows, ext_cols)).astype(
        jnp.bfloat16
    )
    row_ok = (lax.axis_index("gx") > 0) | (lax.broadcasted_iota(jnp.int32, hidden.shape, 0) >= margin)
    col_ok = (lax.axis_index("gy") > 0) | (
        lax.broadcasted_iota(jnp.int32, hidden.shape, 1) >= margin * chans
    )
    hidden = jnp.where(row_ok & col_ok, hidden, jnp.zeros_like(hidden))
    fine = hidden[margin:, margin * chans :]
    for taps, weight in ((dw1, pw1), (dw2, pw2), (dw3, pw3), (dw4, pw4)):
        hidden = strided_kernel(hidden, taps, weight)
    coarse_chans = dwc.shape[2]
    halo = 2 ** (LC - 1) - 1
    grid4 = hidden.reshape(hidden.shape[0], -1, coarse_chans)
    upper = shifted(grid4[-1:], "gx", 1)
    extended = jnp.concatenate([upper, grid4], axis=0)
    leftside = shifted(extended[:, -halo:], "gy", 1)
    extended = jnp.concatenate([leftside, extended], axis=1)
    hidden = strided_cells(extended, dwc[0], pwc[0])
    hidden = lax.all_gather(hidden, "gx", axis=0, tiled=True)
    for level in range(1, LC - 1):
        hidden = strided_cells(pad_top(hidden), dwc[level], pwc[level])
    hidden = lax.all_gather(hidden, "gy", axis=1, tiled=True)
    hidden = strided_cells(pad_left(pad_top(hidden)), dwc[LC - 1], pwc[LC - 1])
    return (fine, hidden.reshape(hidden.shape[0], -1))


def pad_top(cells):
    return jnp.concatenate([jnp.zeros_like(cells[:1]), cells], axis=0)


def pad_left(cells):
    return jnp.concatenate([jnp.zeros_like(cells[:, :1]), cells], axis=1)


def strided_cells(padded, taps, weight):
    rows = (padded.shape[0] - 1) // 2
    cols = (padded.shape[1] - 1) // 2
    total = jnp.zeros((rows, cols, padded.shape[2]), jnp.float32)
    for first in range(3):
        for second in range(3):
            piece = padded[first : first + 2 * rows : 2, second : second + 2 * cols : 2]
            total = total + piece.astype(jnp.float32) * taps[3 * first + second]
    flat = total.astype(jnp.bfloat16).reshape(rows * cols, -1)
    mixed = jnp.dot(flat, weight, preferred_element_type=jnp.float32)
    return gelu_tanh(mixed).astype(jnp.bfloat16).reshape(rows, cols, weight.shape[1])


def solution(mesh):
    placed = (P("gx", "gy"), P(), P(), P(), P(), P(), P(), P(), P(), P(), P(), P(), P())
    return jax.shard_map(
        local, mesh=mesh, in_specs=placed, out_specs=(P("gx", "gy"), P()), check_vma=False
    )
```

```python
import functools

import jax
import jax.numpy as jnp
from jax import lax
from jax.experimental import pallas as pl
from jax.experimental.pallas import tpu as pltpu
from jax.sharding import PartitionSpec as P

LC = 4


def shifted(value, axis, steps):
    count = lax.axis_size(axis)
    leading, last = (max(0, -steps), min(count, count - steps))
    return lax.ppermute(value, axis, [(source, source + steps) for source in range(leading, last)])


def padded_2(block, sides, width):
    for axis, dim in sides:
        count = lax.axis_size(axis)
        forward = [(i, i + 1) for i in range(count - 1)]
        backward = [(target, source) for source, target in forward]
        low = lax.ppermute(
            lax.slice_in_dim(block, block.shape[dim] - width, None, axis=dim), axis, forward
        )
        high = lax.ppermute(lax.slice_in_dim(block, 0, width, axis=dim), axis, backward)
        block = jnp.concatenate([low, block, high], axis=dim)
    return block


def gelu_tanh(value):
    return jax.nn.gelu(value, approximate=True)


def point_flat(spread, weight, rows, cols):
    chans = weight.shape[0]
    flat = spread.astype(jnp.bfloat16).reshape(rows * cols, chans)
    mixed = jnp.dot(flat, weight, preferred_element_type=jnp.float32)
    return gelu_tanh(mixed).reshape(rows, cols * weight.shape[1])


def down_level(field, taps, weight, split_rows, split_cols):
    chans = taps.shape[1]
    rows = field.shape[0]
    cols = field.shape[1] // chans
    half_rows = rows // 2
    half_cols = cols // 2
    if split_rows:
        upper = shifted(field[-1:], "gx", 1)
    else:
        upper = jnp.zeros((1, cols * chans), jnp.bfloat16)
    extended = jnp.concatenate([upper, field], axis=0)
    if split_cols:
        leftside = shifted(extended[:, -chans:], "gy", 1)
    else:
        leftside = jnp.zeros((rows + 1, chans), jnp.bfloat16)
    tiled = jnp.tile(taps, (1, half_cols))
    total = jnp.zeros((half_rows, half_cols * chans), jnp.float32)
    for first in range(3):
        slab = extended[first : first + rows : 2]
        left_slab = leftside[first : first + rows : 2]
        pairs = slab.reshape(half_rows, half_cols, 2 * chans)
        even_cells = pairs[:, :, :chans].reshape(half_rows, half_cols * chans)
        odd_cells = pairs[:, :, chans:].reshape(half_rows, half_cols * chans)
        before = jnp.concatenate([left_slab, odd_cells[:, :-chans]], axis=1)
        for second, piece in enumerate((before, even_cells, odd_cells)):
            total = total + piece.astype(jnp.float32) * tiled[3 * first + second]
    return point_flat(total, weight, half_rows, half_cols).astype(jnp.bfloat16)


def strided_flat(ext, taps, weight):
    chans = taps.shape[1]
    rows = (ext.shape[0] - 1) // 2
    cols = (ext.shape[1] // chans - 1) // 2
    tiled = jnp.tile(taps, (1, cols))
    total = jnp.zeros((rows, cols * chans), jnp.float32)
    for first in range(3):
        slab = ext[first : first + 2 * rows : 2]
        head = slab[:, : 2 * cols * chans].reshape(rows, cols, 2 * chans)
        tail = slab[:, chans:].reshape(rows, cols, 2 * chans)
        pieces = (head[:, :, :chans], head[:, :, chans:], tail[:, :, chans:])
        for second, piece in enumerate(pieces):
            piece = piece.reshape(rows, cols * chans)
            total = total + piece.astype(jnp.float32) * tiled[3 * first + second]
    return point_flat(total, weight, rows, cols).astype(jnp.bfloat16)


def pair_kernel(even_ref, odd_ref, near_ref, far_ref, w_ref, o_ref, *, rows, chans, chunk, width):
    lanes = even_ref.shape[1]
    slabs = [even_ref[pl.ds(0, rows), :], odd_ref[...], even_ref[pl.ds(1, rows), :]]
    aheads = [pltpu.roll(slab, lanes - 2 * chans, 1) for slab in slabs]
    weight = w_ref[...]
    for index in range(lanes // chunk):
        window = slice(index * chunk, (index + 1) * chunk)
        total = None
        for first in range(3):
            term = (
                slabs[first][:, window] * near_ref[first : first + 1, :]
                + aheads[first][:, window] * far_ref[first : first + 1, :]
            )
            total = term if total is None else total + term
        part = jnp.dot(total.astype(jnp.bfloat16), weight, preferred_element_type=jnp.float32)
        o_ref[:, index * width : (index + 1) * width] = gelu_tanh(part).astype(o_ref.dtype)


def strided_kernel(ext, taps, weight):
    chans = taps.shape[1]
    outs = weight.shape[1]
    rows = (ext.shape[0] - 1) // 2
    cols = (ext.shape[1] // chans - 1) // 2
    pairs = cols + 1
    if pairs * 2 * chans % 128:
        pairs += 1
    padded_rows = -(-rows // 8) * 8
    lanes = pairs * 2 * chans
    source = jnp.pad(
        ext.astype(jnp.float32),
        ((0, 2 * padded_rows + 1 - ext.shape[0]), (0, lanes - ext.shape[1])),
    )
    chunk = max(128, 2 * chans)
    group = chunk // (2 * chans)
    grouped = taps.reshape(3, 3, chans)
    near = jnp.tile(grouped[:, :2].reshape(3, 2 * chans), (1, group))
    far = jnp.tile(
        jnp.concatenate([grouped[:, 2:], jnp.zeros_like(grouped[:, 2:])], axis=1).reshape(3, 2 * chans),
        (1, group),
    )
    doubled = jnp.concatenate([weight, weight], axis=0)
    block = jnp.kron(jnp.eye(group, dtype=weight.dtype), doubled) if group > 1 else doubled
    width = group * outs
    body = functools.partial(pair_kernel, rows=padded_rows, chans=chans, chunk=chunk, width=width)
    result = pl.pallas_call(
        body,
        out_shape=jax.ShapeDtypeStruct((padded_rows, pairs * outs), jnp.bfloat16),
    )(source[0::2], source[1::2], near, far, block)
    return result[:rows, : cols * outs]


def local(field, dw0, pw0, dw1, pw1, dw2, pw2, dw3, pw3, dw4, pw4, dwc, pwc):
    chans = dw0.shape[1]
    rows = field.shape[0]
    cols = field.shape[1] // chans
    depth = 4
    margin = 2**depth - 1
    upper = shifted(field[-margin - 2 :], "gx", 1)
    lower = shifted(field[:2], "gx", -1)
    stacked = jnp.concatenate([upper, field, lower], axis=0)
    leftside = shifted(stacked[:, -(margin + 2) * chans :], "gy", 1)
    rightside = shifted(stacked[:, : 2 * chans], "gy", -1)
    flat_pad = jnp.concatenate([leftside, stacked, rightside], axis=1)
    ext_rows = rows + margin
    ext_cols = cols + margin
    tiled = jnp.tile(dw0, (1, ext_cols))
    total = jnp.zeros((ext_rows, ext_cols * chans), jnp.float32)
    for first in range(3):
        for second in range(3):
            piece = flat_pad[
                2 * first : 2 * first + ext_rows,
                2 * second * chans : 2 * second * chans + ext_cols * chans,
            ]
            total = total + piece.astype(jnp.float32) * tiled[3 * first + second]
    centre = flat_pad[2 : 2 + ext_rows, 2 * chans : 2 * chans + ext_cols * chans]
    hidden = (centre.astype(jnp.float32) + point_flat(total, pw0, ext_rows, ext_cols)).astype(
        jnp.bfloat16
    )
    row_ok = (lax.axis_index("gx") > 0) | (lax.broadcasted_iota(jnp.int32, hidden.shape, 0) >= margin)
    col_ok = (lax.axis_index("gy") > 0) | (
        lax.broadcasted_iota(jnp.int32, hidden.shape, 1) >= margin * chans
    )
    hidden = jnp.where(row_ok & col_ok, hidden, jnp.zeros_like(hidden))
    fine = hidden[margin:, margin * chans :]
    for taps, weight in ((dw1, pw1), (dw2, pw2), (dw3, pw3), (dw4, pw4)):
        hidden = strided_kernel(hidden, taps, weight)
    coarse_chans = dwc.shape[2]
    halo = 2 ** (LC - 1) - 1
    grid4 = hidden.reshape(hidden.shape[0], -1, coarse_chans)
    upper = shifted(grid4[-1:], "gx", 1)
    extended = jnp.concatenate([upper, grid4], axis=0)
    leftside = shifted(extended[:, -halo:], "gy", 1)
    extended = jnp.concatenate([leftside, extended], axis=1)
    hidden = strided_cells(extended, dwc[0], pwc[0])
    hidden = lax.all_gather(hidden, "gx", axis=0, tiled=True)
    for level in range(1, LC - 1):
        hidden = strided_cells(pad_top(hidden), dwc[level], pwc[level])
    hidden = lax.all_gather(hidden, "gy", axis=1, tiled=True)
    hidden = strided_cells(pad_left(pad_top(hidden)), dwc[LC - 1], pwc[LC - 1])
    return (fine, hidden.reshape(hidden.shape[0], -1))


def pad_top(cells):
    return jnp.concatenate([jnp.zeros_like(cells[:1]), cells], axis=0)


def pad_left(cells):
    return jnp.concatenate([jnp.zeros_like(cells[:, :1]), cells], axis=1)


def strided_cells(padded, taps, weight):
    rows = (padded.shape[0] - 1) // 2
    cols = (padded.shape[1] - 1) // 2
    total = jnp.zeros((rows, cols, padded.shape[2]), jnp.float32)
    for first in range(3):
        for second in range(3):
            piece = padded[first : first + 2 * rows : 2, second : second + 2 * cols : 2]
            total = total + piece.astype(jnp.float32) * taps[3 * first + second]
    flat = total.astype(jnp.bfloat16).reshape(rows * cols, -1)
    mixed = jnp.dot(flat, weight, preferred_element_type=jnp.float32)
    return gelu_tanh(mixed).astype(jnp.bfloat16).reshape(rows, cols, weight.shape[1])


def solution(mesh):
    placed = (P("gx", "gy"), P(), P(), P(), P(), P(), P(), P(), P(), P(), P(), P(), P())
    return jax.shard_map(
        local, mesh=mesh, in_specs=placed, out_specs=(P("gx", "gy"), P()), check_vma=False
    )
```

```python
import functools

import jax
import jax.numpy as jnp
from jax import lax
from jax.experimental import pallas as pl
from jax.experimental.pallas import tpu as pltpu
from jax.sharding import PartitionSpec as P

LC = 4


def shifted(value, axis, steps):
    count = lax.axis_size(axis)
    leading, last = (max(0, -steps), min(count, count - steps))
    return lax.ppermute(value, axis, [(source, source + steps) for source in range(leading, last)])


def padded_2(block, sides, width):
    for axis, dim in sides:
        count = lax.axis_size(axis)
        forward = [(i, i + 1) for i in range(count - 1)]
        backward = [(target, source) for source, target in forward]
        low = lax.ppermute(
            lax.slice_in_dim(block, block.shape[dim] - width, None, axis=dim), axis, forward
        )
        high = lax.ppermute(lax.slice_in_dim(block, 0, width, axis=dim), axis, backward)
        block = jnp.concatenate([low, block, high], axis=dim)
    return block


def gelu_tanh(value):
    return jax.nn.gelu(value, approximate=True)


def point_flat(spread, weight, rows, cols):
    chans = weight.shape[0]
    flat = spread.astype(jnp.bfloat16).reshape(rows * cols, chans)
    mixed = jnp.dot(flat, weight, preferred_element_type=jnp.float32)
    return gelu_tanh(mixed).reshape(rows, cols * weight.shape[1])


def down_level(field, taps, weight, split_rows, split_cols):
    chans = taps.shape[1]
    rows = field.shape[0]
    cols = field.shape[1] // chans
    half_rows = rows // 2
    half_cols = cols // 2
    if split_rows:
        upper = shifted(field[-1:], "gx", 1)
    else:
        upper = jnp.zeros((1, cols * chans), jnp.bfloat16)
    extended = jnp.concatenate([upper, field], axis=0)
    if split_cols:
        leftside = shifted(extended[:, -chans:], "gy", 1)
    else:
        leftside = jnp.zeros((rows + 1, chans), jnp.bfloat16)
    tiled = jnp.tile(taps, (1, half_cols))
    total = jnp.zeros((half_rows, half_cols * chans), jnp.float32)
    for first in range(3):
        slab = extended[first : first + rows : 2]
        left_slab = leftside[first : first + rows : 2]
        pairs = slab.reshape(half_rows, half_cols, 2 * chans)
        even_cells = pairs[:, :, :chans].reshape(half_rows, half_cols * chans)
        odd_cells = pairs[:, :, chans:].reshape(half_rows, half_cols * chans)
        before = jnp.concatenate([left_slab, odd_cells[:, :-chans]], axis=1)
        for second, piece in enumerate((before, even_cells, odd_cells)):
            total = total + piece.astype(jnp.float32) * tiled[3 * first + second]
    return point_flat(total, weight, half_rows, half_cols).astype(jnp.bfloat16)


def strided_flat(ext, taps, weight):
    chans = taps.shape[1]
    rows = (ext.shape[0] - 1) // 2
    cols = (ext.shape[1] // chans - 1) // 2
    tiled = jnp.tile(taps, (1, cols))
    total = jnp.zeros((rows, cols * chans), jnp.float32)
    for first in range(3):
        slab = ext[first : first + 2 * rows : 2]
        head = slab[:, : 2 * cols * chans].reshape(rows, cols, 2 * chans)
        tail = slab[:, chans:].reshape(rows, cols, 2 * chans)
        pieces = (head[:, :, :chans], head[:, :, chans:], tail[:, :, chans:])
        for second, piece in enumerate(pieces):
            piece = piece.reshape(rows, cols * chans)
            total = total + piece.astype(jnp.float32) * tiled[3 * first + second]
    return point_flat(total, weight, rows, cols).astype(jnp.bfloat16)


def pair_kernel(even_ref, odd_ref, near_ref, far_ref, w_ref, o_ref, *, rows, chans, chunk, width):
    lanes = even_ref.shape[1]
    slabs = [even_ref[pl.ds(0, rows), :], odd_ref[...], even_ref[pl.ds(1, rows), :]]
    aheads = [pltpu.roll(slab, lanes - 2 * chans, 1) for slab in slabs]
    weight = w_ref[...]
    for index in range(lanes // chunk):
        window = slice(index * chunk, (index + 1) * chunk)
        total = None
        for first in range(3):
            term = (
                slabs[first][:, window] * near_ref[first : first + 1, :]
                + aheads[first][:, window] * far_ref[first : first + 1, :]
            )
            total = term if total is None else total + term
        part = jnp.dot(total.astype(jnp.bfloat16), weight, preferred_element_type=jnp.float32)
        o_ref[:, index * width : (index + 1) * width] = gelu_tanh(part).astype(o_ref.dtype)


def prepare(taps, weight):
    chans = taps.shape[1]
    chunk = max(128, 2 * chans)
    group = chunk // (2 * chans)
    grouped = taps.reshape(3, 3, chans)
    near = jnp.tile(grouped[:, :2].reshape(3, 2 * chans), (1, group))
    far = jnp.tile(
        jnp.concatenate([grouped[:, 2:], jnp.zeros_like(grouped[:, 2:])], axis=1).reshape(3, 2 * chans),
        (1, group),
    )
    doubled = jnp.concatenate([weight, weight], axis=0)
    block = jnp.kron(jnp.eye(group, dtype=weight.dtype), doubled) if group > 1 else doubled
    return near, far, block


def strided_kernel(ext, chans, outs, prepared):
    near, far, block = prepared
    rows = (ext.shape[0] - 1) // 2
    cols = (ext.shape[1] // chans - 1) // 2
    pairs = cols + 1
    if pairs * 2 * chans % 128:
        pairs += 1
    padded_rows = -(-rows // 8) * 8
    lanes = pairs * 2 * chans
    source = jnp.pad(
        ext.astype(jnp.float32),
        ((0, 2 * padded_rows + 1 - ext.shape[0]), (0, lanes - ext.shape[1])),
    )
    chunk = max(128, 2 * chans)
    group = chunk // (2 * chans)
    width = group * outs
    body = functools.partial(pair_kernel, rows=padded_rows, chans=chans, chunk=chunk, width=width)
    result = pl.pallas_call(
        body,
        out_shape=jax.ShapeDtypeStruct((padded_rows, pairs * outs), jnp.bfloat16),
    )(source[0::2], source[1::2], near, far, block)
    return result[:rows, : cols * outs]


def local(field, dw0, pw0, dw1, pw1, dw2, pw2, dw3, pw3, dw4, pw4, dwc, pwc):
    chans = dw0.shape[1]
    rows = field.shape[0]
    cols = field.shape[1] // chans
    depth = 4
    margin = 2**depth - 1
    upper = shifted(field[-margin - 2 :], "gx", 1)
    lower = shifted(field[:2], "gx", -1)
    stacked = jnp.concatenate([upper, field, lower], axis=0)
    params = ((dw1, pw1), (dw2, pw2), (dw3, pw3), (dw4, pw4))
    params, stacked = lax.optimization_barrier((params, stacked))
    leftside = shifted(stacked[:, -(margin + 2) * chans :], "gy", 1)
    rightside = shifted(stacked[:, : 2 * chans], "gy", -1)
    flat_pad = jnp.concatenate([leftside, stacked, rightside], axis=1)
    ext_rows = rows + margin
    ext_cols = cols + margin
    tiled = jnp.tile(dw0, (1, ext_cols))
    total = jnp.zeros((ext_rows, ext_cols * chans), jnp.float32)
    for first in range(3):
        for second in range(3):
            piece = flat_pad[
                2 * first : 2 * first + ext_rows,
                2 * second * chans : 2 * second * chans + ext_cols * chans,
            ]
            total = total + piece.astype(jnp.float32) * tiled[3 * first + second]
    centre = flat_pad[2 : 2 + ext_rows, 2 * chans : 2 * chans + ext_cols * chans]
    hidden = (centre.astype(jnp.float32) + point_flat(total, pw0, ext_rows, ext_cols)).astype(
        jnp.bfloat16
    )
    row_ok = (lax.axis_index("gx") > 0) | (lax.broadcasted_iota(jnp.int32, hidden.shape, 0) >= margin)
    col_ok = (lax.axis_index("gy") > 0) | (
        lax.broadcasted_iota(jnp.int32, hidden.shape, 1) >= margin * chans
    )
    hidden = jnp.where(row_ok & col_ok, hidden, jnp.zeros_like(hidden))
    fine = hidden[margin:, margin * chans :]
    for taps, weight in params:
        prepared = prepare(taps, weight)
        hidden = strided_kernel(hidden, taps.shape[1], weight.shape[1], prepared)
    coarse_chans = dwc.shape[2]
    halo = 2 ** (LC - 1) - 1
    grid4 = hidden.reshape(hidden.shape[0], -1, coarse_chans)
    upper = shifted(grid4[-1:], "gx", 1)
    extended = jnp.concatenate([upper, grid4], axis=0)
    leftside = shifted(extended[:, -halo:], "gy", 1)
    extended = jnp.concatenate([leftside, extended], axis=1)
    hidden = strided_cells(extended, dwc[0], pwc[0])
    hidden = lax.all_gather(hidden, "gx", axis=0, tiled=True)
    for level in range(1, LC - 1):
        hidden = strided_cells(pad_top(hidden), dwc[level], pwc[level])
    hidden = lax.all_gather(hidden, "gy", axis=1, tiled=True)
    hidden = strided_cells(pad_left(pad_top(hidden)), dwc[LC - 1], pwc[LC - 1])
    return (fine, hidden.reshape(hidden.shape[0], -1))


def pad_top(cells):
    return jnp.concatenate([jnp.zeros_like(cells[:1]), cells], axis=0)


def pad_left(cells):
    return jnp.concatenate([jnp.zeros_like(cells[:, :1]), cells], axis=1)


def strided_cells(padded, taps, weight):
    rows = (padded.shape[0] - 1) // 2
    cols = (padded.shape[1] - 1) // 2
    total = jnp.zeros((rows, cols, padded.shape[2]), jnp.float32)
    for first in range(3):
        for second in range(3):
            piece = padded[first : first + 2 * rows : 2, second : second + 2 * cols : 2]
            total = total + piece.astype(jnp.float32) * taps[3 * first + second]
    flat = total.astype(jnp.bfloat16).reshape(rows * cols, -1)
    mixed = jnp.dot(flat, weight, preferred_element_type=jnp.float32)
    return gelu_tanh(mixed).astype(jnp.bfloat16).reshape(rows, cols, weight.shape[1])


def solution(mesh):
    placed = (P("gx", "gy"), P(), P(), P(), P(), P(), P(), P(), P(), P(), P(), P(), P())
    return jax.shard_map(
        local, mesh=mesh, in_specs=placed, out_specs=(P("gx", "gy"), P()), check_vma=False
    )
```

```python
import functools

import jax
import jax.numpy as jnp
from jax import lax
from jax.experimental import pallas as pl
from jax.experimental.pallas import tpu as pltpu
from jax.sharding import PartitionSpec as P

LC = 4


def shifted(value, axis, steps):
    count = lax.axis_size(axis)
    leading, last = (max(0, -steps), min(count, count - steps))
    return lax.ppermute(value, axis, [(source, source + steps) for source in range(leading, last)])


def padded_2(block, sides, width):
    for axis, dim in sides:
        count = lax.axis_size(axis)
        forward = [(i, i + 1) for i in range(count - 1)]
        backward = [(target, source) for source, target in forward]
        low = lax.ppermute(
            lax.slice_in_dim(block, block.shape[dim] - width, None, axis=dim), axis, forward
        )
        high = lax.ppermute(lax.slice_in_dim(block, 0, width, axis=dim), axis, backward)
        block = jnp.concatenate([low, block, high], axis=dim)
    return block


def gelu_tanh(value):
    return jax.nn.gelu(value, approximate=True)


def point_flat(spread, weight, rows, cols):
    chans = weight.shape[0]
    flat = spread.astype(jnp.bfloat16).reshape(rows * cols, chans)
    mixed = jnp.dot(flat, weight, preferred_element_type=jnp.float32)
    return gelu_tanh(mixed).reshape(rows, cols * weight.shape[1])


def down_level(field, taps, weight, split_rows, split_cols):
    chans = taps.shape[1]
    rows = field.shape[0]
    cols = field.shape[1] // chans
    half_rows = rows // 2
    half_cols = cols // 2
    if split_rows:
        upper = shifted(field[-1:], "gx", 1)
    else:
        upper = jnp.zeros((1, cols * chans), jnp.bfloat16)
    extended = jnp.concatenate([upper, field], axis=0)
    if split_cols:
        leftside = shifted(extended[:, -chans:], "gy", 1)
    else:
        leftside = jnp.zeros((rows + 1, chans), jnp.bfloat16)
    tiled = jnp.tile(taps, (1, half_cols))
    total = jnp.zeros((half_rows, half_cols * chans), jnp.float32)
    for first in range(3):
        slab = extended[first : first + rows : 2]
        left_slab = leftside[first : first + rows : 2]
        pairs = slab.reshape(half_rows, half_cols, 2 * chans)
        even_cells = pairs[:, :, :chans].reshape(half_rows, half_cols * chans)
        odd_cells = pairs[:, :, chans:].reshape(half_rows, half_cols * chans)
        before = jnp.concatenate([left_slab, odd_cells[:, :-chans]], axis=1)
        for second, piece in enumerate((before, even_cells, odd_cells)):
            total = total + piece.astype(jnp.float32) * tiled[3 * first + second]
    return point_flat(total, weight, half_rows, half_cols).astype(jnp.bfloat16)


def strided_flat(ext, taps, weight):
    chans = taps.shape[1]
    rows = (ext.shape[0] - 1) // 2
    cols = (ext.shape[1] // chans - 1) // 2
    tiled = jnp.tile(taps, (1, cols))
    total = jnp.zeros((rows, cols * chans), jnp.float32)
    for first in range(3):
        slab = ext[first : first + 2 * rows : 2]
        head = slab[:, : 2 * cols * chans].reshape(rows, cols, 2 * chans)
        tail = slab[:, chans:].reshape(rows, cols, 2 * chans)
        pieces = (head[:, :, :chans], head[:, :, chans:], tail[:, :, chans:])
        for second, piece in enumerate(pieces):
            piece = piece.reshape(rows, cols * chans)
            total = total + piece.astype(jnp.float32) * tiled[3 * first + second]
    return point_flat(total, weight, rows, cols).astype(jnp.bfloat16)


def prepare(taps, weight):
    chans = taps.shape[1]
    chunk = max(128, 2 * chans)
    group = chunk // (2 * chans)
    grouped = taps.reshape(3, 3, chans)
    near = jnp.tile(grouped[:, :2].reshape(3, 2 * chans), (1, group))
    far = jnp.tile(
        jnp.concatenate([grouped[:, 2:], jnp.zeros_like(grouped[:, 2:])], axis=1).reshape(3, 2 * chans),
        (1, group),
    )
    doubled = jnp.concatenate([weight, weight], axis=0)
    block = jnp.kron(jnp.eye(group, dtype=weight.dtype), doubled) if group > 1 else doubled
    return near, far, block


def chain_kernel(*refs, plan):
    x_ref = refs[0]
    o_ref = refs[-1]
    value = x_ref[...].astype(jnp.float32)
    lanes = value.shape[1]
    for level, (valid, rows, chans, outs) in enumerate(plan):
        near_ref, far_ref, w_ref = refs[1 + 3 * level : 4 + 3 * level]
        shape = (rows, value.shape[0])
        out_row = lax.broadcasted_iota(jnp.int32, shape, 0)
        in_row = lax.broadcasted_iota(jnp.int32, shape, 1)
        slabs = []
        for first in range(3):
            pick = ((in_row == 2 * out_row + first) & (in_row < valid)).astype(jnp.float32)
            slabs.append(jnp.dot(pick, value, preferred_element_type=jnp.float32))
        aheads = [pltpu.roll(slab, lanes - 2 * chans, 1) for slab in slabs]
        weight = w_ref[...]
        chunk = max(128, 2 * chans)
        width = weight.shape[1]
        parts = []
        for index in range(lanes // chunk):
            window = slice(index * chunk, (index + 1) * chunk)
            total = None
            for first in range(3):
                term = (
                    slabs[first][:, window] * near_ref[first : first + 1, :]
                    + aheads[first][:, window] * far_ref[first : first + 1, :]
                )
                total = term if total is None else total + term
            part = jnp.dot(total.astype(jnp.bfloat16), weight, preferred_element_type=jnp.float32)
            parts.append(gelu_tanh(part).astype(jnp.bfloat16))
        value = jnp.concatenate(parts, axis=1).astype(jnp.float32)
    o_ref[...] = value.astype(o_ref.dtype)


def strided_chain(ext, chans, params):
    rows = ext.shape[0]
    cols = ext.shape[1] // chans
    plan = []
    operands = []
    lanes = None
    for taps, weight in params:
        out_rows = (rows - 1) // 2
        out_cols = (cols - 1) // 2
        pairs = out_cols + 1
        if pairs * 2 * chans % 128:
            pairs += 1
        lanes = lanes or pairs * 2 * chans
        plan.append((rows, -(-out_rows // 8) * 8, chans, weight.shape[1]))
        operands.extend(prepare(taps, weight))
        rows, cols, chans = out_rows, out_cols, weight.shape[1]
    source = jnp.pad(ext, ((0, -ext.shape[0] % 8), (0, lanes - ext.shape[1])))
    result = pl.pallas_call(
        functools.partial(chain_kernel, plan=tuple(plan)),
        out_shape=jax.ShapeDtypeStruct((plan[-1][1], lanes), jnp.bfloat16),
    )(source, *operands)
    return result[:rows, : cols * chans]


def local(field, dw0, pw0, dw1, pw1, dw2, pw2, dw3, pw3, dw4, pw4, dwc, pwc):
    chans = dw0.shape[1]
    rows = field.shape[0]
    cols = field.shape[1] // chans
    depth = 4
    margin = 2**depth - 1
    upper = shifted(field[-margin - 2 :], "gx", 1)
    lower = shifted(field[:2], "gx", -1)
    stacked = jnp.concatenate([upper, field, lower], axis=0)
    params = ((dw1, pw1), (dw2, pw2), (dw3, pw3), (dw4, pw4))
    params, stacked = lax.optimization_barrier((params, stacked))
    leftside = shifted(stacked[:, -(margin + 2) * chans :], "gy", 1)
    rightside = shifted(stacked[:, : 2 * chans], "gy", -1)
    flat_pad = jnp.concatenate([leftside, stacked, rightside], axis=1)
    ext_rows = rows + margin
    ext_cols = cols + margin
    tiled = jnp.tile(dw0, (1, ext_cols))
    total = jnp.zeros((ext_rows, ext_cols * chans), jnp.float32)
    for first in range(3):
        for second in range(3):
            piece = flat_pad[
                2 * first : 2 * first + ext_rows,
                2 * second * chans : 2 * second * chans + ext_cols * chans,
            ]
            total = total + piece.astype(jnp.float32) * tiled[3 * first + second]
    centre = flat_pad[2 : 2 + ext_rows, 2 * chans : 2 * chans + ext_cols * chans]
    hidden = (centre.astype(jnp.float32) + point_flat(total, pw0, ext_rows, ext_cols)).astype(
        jnp.bfloat16
    )
    row_ok = (lax.axis_index("gx") > 0) | (lax.broadcasted_iota(jnp.int32, hidden.shape, 0) >= margin)
    col_ok = (lax.axis_index("gy") > 0) | (
        lax.broadcasted_iota(jnp.int32, hidden.shape, 1) >= margin * chans
    )
    hidden = jnp.where(row_ok & col_ok, hidden, jnp.zeros_like(hidden))
    fine = hidden[margin:, margin * chans :]
    hidden = strided_chain(hidden, chans, params)
    coarse_chans = dwc.shape[2]
    halo = 2 ** (LC - 1) - 1
    grid4 = hidden.reshape(hidden.shape[0], -1, coarse_chans)
    upper = shifted(grid4[-1:], "gx", 1)
    extended = jnp.concatenate([upper, grid4], axis=0)
    leftside = shifted(extended[:, -halo:], "gy", 1)
    extended = jnp.concatenate([leftside, extended], axis=1)
    hidden = strided_cells(extended, dwc[0], pwc[0])
    hidden = lax.all_gather(hidden, "gx", axis=0, tiled=True)
    for level in range(1, LC - 1):
        hidden = strided_cells(pad_top(hidden), dwc[level], pwc[level])
    hidden = lax.all_gather(hidden, "gy", axis=1, tiled=True)
    hidden = strided_cells(pad_left(pad_top(hidden)), dwc[LC - 1], pwc[LC - 1])
    return (fine, hidden.reshape(hidden.shape[0], -1))


def pad_top(cells):
    return jnp.concatenate([jnp.zeros_like(cells[:1]), cells], axis=0)


def pad_left(cells):
    return jnp.concatenate([jnp.zeros_like(cells[:, :1]), cells], axis=1)


def strided_cells(padded, taps, weight):
    rows = (padded.shape[0] - 1) // 2
    cols = (padded.shape[1] - 1) // 2
    total = jnp.zeros((rows, cols, padded.shape[2]), jnp.float32)
    for first in range(3):
        for second in range(3):
            piece = padded[first : first + 2 * rows : 2, second : second + 2 * cols : 2]
            total = total + piece.astype(jnp.float32) * taps[3 * first + second]
    flat = total.astype(jnp.bfloat16).reshape(rows * cols, -1)
    mixed = jnp.dot(flat, weight, preferred_element_type=jnp.float32)
    return gelu_tanh(mixed).astype(jnp.bfloat16).reshape(rows, cols, weight.shape[1])


def solution(mesh):
    placed = (P("gx", "gy"), P(), P(), P(), P(), P(), P(), P(), P(), P(), P(), P(), P())
    return jax.shard_map(
        local, mesh=mesh, in_specs=placed, out_specs=(P("gx", "gy"), P()), check_vma=False
    )
```

```python
import functools

import jax
import jax.numpy as jnp
from jax import lax
from jax.experimental import pallas as pl
from jax.experimental.pallas import tpu as pltpu
from jax.sharding import PartitionSpec as P

LC = 4


def shifted(value, axis, steps):
    count = lax.axis_size(axis)
    leading, last = (max(0, -steps), min(count, count - steps))
    return lax.ppermute(value, axis, [(source, source + steps) for source in range(leading, last)])


def padded_2(block, sides, width):
    for axis, dim in sides:
        count = lax.axis_size(axis)
        forward = [(i, i + 1) for i in range(count - 1)]
        backward = [(target, source) for source, target in forward]
        low = lax.ppermute(
            lax.slice_in_dim(block, block.shape[dim] - width, None, axis=dim), axis, forward
        )
        high = lax.ppermute(lax.slice_in_dim(block, 0, width, axis=dim), axis, backward)
        block = jnp.concatenate([low, block, high], axis=dim)
    return block


def gelu_tanh(value):
    return jax.nn.gelu(value, approximate=True)


def point_flat(spread, weight, rows, cols):
    chans = weight.shape[0]
    flat = spread.astype(jnp.bfloat16).reshape(rows * cols, chans)
    mixed = jnp.dot(flat, weight, preferred_element_type=jnp.float32)
    return gelu_tanh(mixed).reshape(rows, cols * weight.shape[1])


def down_level(field, taps, weight, split_rows, split_cols):
    chans = taps.shape[1]
    rows = field.shape[0]
    cols = field.shape[1] // chans
    half_rows = rows // 2
    half_cols = cols // 2
    if split_rows:
        upper = shifted(field[-1:], "gx", 1)
    else:
        upper = jnp.zeros((1, cols * chans), jnp.bfloat16)
    extended = jnp.concatenate([upper, field], axis=0)
    if split_cols:
        leftside = shifted(extended[:, -chans:], "gy", 1)
    else:
        leftside = jnp.zeros((rows + 1, chans), jnp.bfloat16)
    tiled = jnp.tile(taps, (1, half_cols))
    total = jnp.zeros((half_rows, half_cols * chans), jnp.float32)
    for first in range(3):
        slab = extended[first : first + rows : 2]
        left_slab = leftside[first : first + rows : 2]
        pairs = slab.reshape(half_rows, half_cols, 2 * chans)
        even_cells = pairs[:, :, :chans].reshape(half_rows, half_cols * chans)
        odd_cells = pairs[:, :, chans:].reshape(half_rows, half_cols * chans)
        before = jnp.concatenate([left_slab, odd_cells[:, :-chans]], axis=1)
        for second, piece in enumerate((before, even_cells, odd_cells)):
            total = total + piece.astype(jnp.float32) * tiled[3 * first + second]
    return point_flat(total, weight, half_rows, half_cols).astype(jnp.bfloat16)


def strided_flat(ext, taps, weight):
    chans = taps.shape[1]
    rows = (ext.shape[0] - 1) // 2
    cols = (ext.shape[1] // chans - 1) // 2
    tiled = jnp.tile(taps, (1, cols))
    total = jnp.zeros((rows, cols * chans), jnp.float32)
    for first in range(3):
        slab = ext[first : first + 2 * rows : 2]
        head = slab[:, : 2 * cols * chans].reshape(rows, cols, 2 * chans)
        tail = slab[:, chans:].reshape(rows, cols, 2 * chans)
        pieces = (head[:, :, :chans], head[:, :, chans:], tail[:, :, chans:])
        for second, piece in enumerate(pieces):
            piece = piece.reshape(rows, cols * chans)
            total = total + piece.astype(jnp.float32) * tiled[3 * first + second]
    return point_flat(total, weight, rows, cols).astype(jnp.bfloat16)


def prepare(taps, weight):
    chans = taps.shape[1]
    chunk = max(128, 2 * chans)
    group = chunk // (2 * chans)
    grouped = taps.reshape(3, 3, chans)
    near = jnp.tile(grouped[:, :2].reshape(3, 2 * chans), (1, group))
    far = jnp.tile(
        jnp.concatenate([grouped[:, 2:], jnp.zeros_like(grouped[:, 2:])], axis=1).reshape(3, 2 * chans),
        (1, group),
    )
    doubled = jnp.concatenate([weight, weight], axis=0)
    block = jnp.kron(jnp.eye(group, dtype=weight.dtype), doubled) if group > 1 else doubled
    return near, far, block


def chain_kernel(*refs, plan):
    value = refs[0][...].astype(jnp.float32)
    refs[-1][...] = chain_levels(value, refs[1:-1], plan).astype(refs[-1].dtype)


def pick_rows(value, rows, offset, valid):
    shape = (rows, value.shape[0])
    out_row = lax.broadcasted_iota(jnp.int32, shape, 0)
    in_row = lax.broadcasted_iota(jnp.int32, shape, 1)
    pick = ((in_row == offset + out_row) & (in_row < valid)).astype(jnp.float32)
    return jnp.dot(pick, value, preferred_element_type=jnp.float32)


def fine_kernel(*refs, plan, rows, cols, margin, chans):
    x_ref, pat_ref, pw_ref, row_ref, col_ref = refs[:5]
    fine_ref, o_ref = refs[-2:]
    source = x_ref[...].astype(jnp.float32)
    lanes = source.shape[1]
    width = plan[0][0] * 0 + col_ref.shape[1]
    ext_rows = row_ref.shape[0]
    shifted = []
    for first in range(3):
        slab = pick_rows(source, ext_rows, 2 * first, source.shape[0])
        shifted.append(
            [slab if second == 0 else pltpu.roll(slab, lanes - 2 * second * chans, 1) for second in range(3)]
        )
    weight = pw_ref[...]
    parts = []
    for index in range(width // 128):
        window = slice(index * 128, (index + 1) * 128)
        total = None
        for first in range(3):
            for second in range(3):
                term = shifted[first][second][:, window] * pat_ref[3 * first + second : 3 * first + second + 1, :]
                total = term if total is None else total + term
        mixed = gelu_tanh(jnp.dot(total.astype(jnp.bfloat16), weight, preferred_element_type=jnp.float32))
        parts.append((shifted[1][1][:, window] + mixed).astype(jnp.bfloat16))
    hidden = jnp.concatenate(parts, axis=1)
    keep = row_ref[...] * col_ref[...]
    hidden = jnp.where(keep > 0, hidden, jnp.zeros_like(hidden)).astype(jnp.float32)
    inner = pltpu.roll(hidden, width - margin * chans, 1)[:, : cols * chans]
    fine_ref[...] = pick_rows(inner, rows, margin, ext_rows).astype(fine_ref.dtype)
    o_ref[...] = chain_levels(hidden, refs[5:-2], plan).astype(o_ref.dtype)


def chain_levels(value, refs, plan):
    lanes = value.shape[1]
    for level, (valid, rows, chans, outs) in enumerate(plan):
        near_ref, far_ref, w_ref = refs[3 * level : 3 + 3 * level]
        shape = (rows, value.shape[0])
        out_row = lax.broadcasted_iota(jnp.int32, shape, 0)
        in_row = lax.broadcasted_iota(jnp.int32, shape, 1)
        slabs = []
        for first in range(3):
            pick = ((in_row == 2 * out_row + first) & (in_row < valid)).astype(jnp.float32)
            slabs.append(jnp.dot(pick, value, preferred_element_type=jnp.float32))
        aheads = [pltpu.roll(slab, lanes - 2 * chans, 1) for slab in slabs]
        weight = w_ref[...]
        chunk = max(128, 2 * chans)
        width = weight.shape[1]
        parts = []
        for index in range(lanes // chunk):
            window = slice(index * chunk, (index + 1) * chunk)
            total = None
            for first in range(3):
                term = (
                    slabs[first][:, window] * near_ref[first : first + 1, :]
                    + aheads[first][:, window] * far_ref[first : first + 1, :]
                )
                total = term if total is None else total + term
            part = jnp.dot(total.astype(jnp.bfloat16), weight, preferred_element_type=jnp.float32)
            parts.append(gelu_tanh(part).astype(jnp.bfloat16))
        value = jnp.concatenate(parts, axis=1).astype(jnp.float32)
    return value


def chain_plan(rows, cols, chans, params):
    plan = []
    operands = []
    lanes = None
    for taps, weight in params:
        out_rows = (rows - 1) // 2
        out_cols = (cols - 1) // 2
        pairs = out_cols + 1
        if pairs * 2 * chans % 128:
            pairs += 1
        lanes = lanes or pairs * 2 * chans
        plan.append((rows, -(-out_rows // 8) * 8, chans, weight.shape[1]))
        operands.extend(prepare(taps, weight))
        rows, cols, chans = out_rows, out_cols, weight.shape[1]
    return tuple(plan), operands, lanes, (rows, cols, chans)


def strided_chain(ext, chans, params):
    rows = ext.shape[0]
    cols = ext.shape[1] // chans
    plan = []
    operands = []
    lanes = None
    for taps, weight in params:
        out_rows = (rows - 1) // 2
        out_cols = (cols - 1) // 2
        pairs = out_cols + 1
        if pairs * 2 * chans % 128:
            pairs += 1
        lanes = lanes or pairs * 2 * chans
        plan.append((rows, -(-out_rows // 8) * 8, chans, weight.shape[1]))
        operands.extend(prepare(taps, weight))
        rows, cols, chans = out_rows, out_cols, weight.shape[1]
    source = jnp.pad(ext, ((0, -ext.shape[0] % 8), (0, lanes - ext.shape[1])))
    result = pl.pallas_call(
        functools.partial(chain_kernel, plan=tuple(plan)),
        out_shape=jax.ShapeDtypeStruct((plan[-1][1], lanes), jnp.bfloat16),
    )(source, *operands)
    return result[:rows, : cols * chans]


def local(field, dw0, pw0, dw1, pw1, dw2, pw2, dw3, pw3, dw4, pw4, dwc, pwc):
    chans = dw0.shape[1]
    rows = field.shape[0]
    cols = field.shape[1] // chans
    depth = 4
    margin = 2**depth - 1
    upper = shifted(field[-margin - 2 :], "gx", 1)
    lower = shifted(field[:2], "gx", -1)
    stacked = jnp.concatenate([upper, field, lower], axis=0)
    params = ((dw1, pw1), (dw2, pw2), (dw3, pw3), (dw4, pw4))
    params, stacked = lax.optimization_barrier((params, stacked))
    leftside = shifted(stacked[:, -(margin + 2) * chans :], "gy", 1)
    rightside = shifted(stacked[:, : 2 * chans], "gy", -1)
    flat_pad = jnp.concatenate([leftside, stacked, rightside], axis=1)
    ext_rows = rows + margin
    ext_cols = cols + margin
    plan, operands, lanes, (last_rows, last_cols, last_chans) = chain_plan(
        ext_rows, ext_cols, chans, params
    )
    padded_rows = -(-ext_rows // 8) * 8
    source = jnp.pad(
        flat_pad,
        (
            (0, padded_rows + 8 - flat_pad.shape[0]),
            (0, lanes + 128 - flat_pad.shape[1]),
        ),
    )
    pattern = jnp.tile(dw0, (1, 128 // chans))
    block = jnp.kron(jnp.eye(128 // chans, dtype=pw0.dtype), pw0)
    row_keep = (
        (lax.axis_index("gx") > 0) | (lax.broadcasted_iota(jnp.int32, (padded_rows, 1), 0) >= margin)
    ).astype(jnp.float32)
    col_keep = (
        (lax.axis_index("gy") > 0) | (lax.broadcasted_iota(jnp.int32, (1, lanes), 1) >= margin * chans)
    ).astype(jnp.float32)
    body = functools.partial(fine_kernel, plan=plan, rows=rows, cols=cols, margin=margin, chans=chans)
    fine, hidden = pl.pallas_call(
        body,
        out_shape=(
            jax.ShapeDtypeStruct((rows, cols * chans), jnp.bfloat16),
            jax.ShapeDtypeStruct((plan[-1][1], lanes), jnp.bfloat16),
        ),
    )(source, pattern, block, row_keep, col_keep, *operands)
    hidden = hidden[:last_rows, : last_cols * last_chans]
    coarse_chans = dwc.shape[2]
    halo = 2 ** (LC - 1) - 1
    grid4 = hidden.reshape(hidden.shape[0], -1, coarse_chans)
    upper = shifted(grid4[-1:], "gx", 1)
    extended = jnp.concatenate([upper, grid4], axis=0)
    leftside = shifted(extended[:, -halo:], "gy", 1)
    extended = jnp.concatenate([leftside, extended], axis=1)
    hidden = strided_cells(extended, dwc[0], pwc[0])
    hidden = lax.all_gather(hidden, "gx", axis=0, tiled=True)
    for level in range(1, LC - 1):
        hidden = strided_cells(pad_top(hidden), dwc[level], pwc[level])
    hidden = lax.all_gather(hidden, "gy", axis=1, tiled=True)
    hidden = strided_cells(pad_left(pad_top(hidden)), dwc[LC - 1], pwc[LC - 1])
    return (fine, hidden.reshape(hidden.shape[0], -1))


def pad_top(cells):
    return jnp.concatenate([jnp.zeros_like(cells[:1]), cells], axis=0)


def pad_left(cells):
    return jnp.concatenate([jnp.zeros_like(cells[:, :1]), cells], axis=1)


def strided_cells(padded, taps, weight):
    rows = (padded.shape[0] - 1) // 2
    cols = (padded.shape[1] - 1) // 2
    total = jnp.zeros((rows, cols, padded.shape[2]), jnp.float32)
    for first in range(3):
        for second in range(3):
            piece = padded[first : first + 2 * rows : 2, second : second + 2 * cols : 2]
            total = total + piece.astype(jnp.float32) * taps[3 * first + second]
    flat = total.astype(jnp.bfloat16).reshape(rows * cols, -1)
    mixed = jnp.dot(flat, weight, preferred_element_type=jnp.float32)
    return gelu_tanh(mixed).astype(jnp.bfloat16).reshape(rows, cols, weight.shape[1])


def solution(mesh):
    placed = (P("gx", "gy"), P(), P(), P(), P(), P(), P(), P(), P(), P(), P(), P(), P())
    return jax.shard_map(
        local, mesh=mesh, in_specs=placed, out_specs=(P("gx", "gy"), P()), check_vma=False
    )
```

```python
import functools

import jax
import jax.numpy as jnp
from jax import lax
from jax.experimental import pallas as pl
from jax.experimental.pallas import tpu as pltpu
from jax.sharding import PartitionSpec as P

LC = 4


def shifted(value, axis, steps):
    count = lax.axis_size(axis)
    leading, last = (max(0, -steps), min(count, count - steps))
    return lax.ppermute(value, axis, [(source, source + steps) for source in range(leading, last)])


def padded_2(block, sides, width):
    for axis, dim in sides:
        count = lax.axis_size(axis)
        forward = [(i, i + 1) for i in range(count - 1)]
        backward = [(target, source) for source, target in forward]
        low = lax.ppermute(
            lax.slice_in_dim(block, block.shape[dim] - width, None, axis=dim), axis, forward
        )
        high = lax.ppermute(lax.slice_in_dim(block, 0, width, axis=dim), axis, backward)
        block = jnp.concatenate([low, block, high], axis=dim)
    return block


def gelu_tanh(value):
    return jax.nn.gelu(value, approximate=True)


def point_flat(spread, weight, rows, cols):
    chans = weight.shape[0]
    flat = spread.astype(jnp.bfloat16).reshape(rows * cols, chans)
    mixed = jnp.dot(flat, weight, preferred_element_type=jnp.float32)
    return gelu_tanh(mixed).reshape(rows, cols * weight.shape[1])


def down_level(field, taps, weight, split_rows, split_cols):
    chans = taps.shape[1]
    rows = field.shape[0]
    cols = field.shape[1] // chans
    half_rows = rows // 2
    half_cols = cols // 2
    if split_rows:
        upper = shifted(field[-1:], "gx", 1)
    else:
        upper = jnp.zeros((1, cols * chans), jnp.bfloat16)
    extended = jnp.concatenate([upper, field], axis=0)
    if split_cols:
        leftside = shifted(extended[:, -chans:], "gy", 1)
    else:
        leftside = jnp.zeros((rows + 1, chans), jnp.bfloat16)
    tiled = jnp.tile(taps, (1, half_cols))
    total = jnp.zeros((half_rows, half_cols * chans), jnp.float32)
    for first in range(3):
        slab = extended[first : first + rows : 2]
        left_slab = leftside[first : first + rows : 2]
        pairs = slab.reshape(half_rows, half_cols, 2 * chans)
        even_cells = pairs[:, :, :chans].reshape(half_rows, half_cols * chans)
        odd_cells = pairs[:, :, chans:].reshape(half_rows, half_cols * chans)
        before = jnp.concatenate([left_slab, odd_cells[:, :-chans]], axis=1)
        for second, piece in enumerate((before, even_cells, odd_cells)):
            total = total + piece.astype(jnp.float32) * tiled[3 * first + second]
    return point_flat(total, weight, half_rows, half_cols).astype(jnp.bfloat16)


def strided_flat(ext, taps, weight):
    chans = taps.shape[1]
    rows = (ext.shape[0] - 1) // 2
    cols = (ext.shape[1] // chans - 1) // 2
    tiled = jnp.tile(taps, (1, cols))
    total = jnp.zeros((rows, cols * chans), jnp.float32)
    for first in range(3):
        slab = ext[first : first + 2 * rows : 2]
        head = slab[:, : 2 * cols * chans].reshape(rows, cols, 2 * chans)
        tail = slab[:, chans:].reshape(rows, cols, 2 * chans)
        pieces = (head[:, :, :chans], head[:, :, chans:], tail[:, :, chans:])
        for second, piece in enumerate(pieces):
            piece = piece.reshape(rows, cols * chans)
            total = total + piece.astype(jnp.float32) * tiled[3 * first + second]
    return point_flat(total, weight, rows, cols).astype(jnp.bfloat16)


def prepare(taps, weight):
    chans = taps.shape[1]
    chunk = max(128, 2 * chans)
    group = chunk // (2 * chans)
    grouped = taps.reshape(3, 3, chans)
    near = jnp.tile(grouped[:, :2].reshape(3, 2 * chans), (1, group))
    far = jnp.tile(
        jnp.concatenate([grouped[:, 2:], jnp.zeros_like(grouped[:, 2:])], axis=1).reshape(3, 2 * chans),
        (1, group),
    )
    doubled = jnp.concatenate([weight, weight], axis=0)
    block = jnp.kron(jnp.eye(group, dtype=weight.dtype), doubled) if group > 1 else doubled
    return near, far, block


def chain_kernel(*refs, plan):
    value = refs[0][...].astype(jnp.float32)
    refs[-1][...] = chain_levels(value, refs[1:-1], plan).astype(refs[-1].dtype)


def pick_rows(value, rows, offset, valid):
    shape = (rows, value.shape[0])
    out_row = lax.broadcasted_iota(jnp.int32, shape, 0)
    in_row = lax.broadcasted_iota(jnp.int32, shape, 1)
    pick = ((in_row == offset + out_row) & (in_row < valid)).astype(jnp.float32)
    return jnp.dot(pick, value, preferred_element_type=jnp.float32)


def fine_kernel(*refs, plan, rows, cols, margin, chans):
    x_ref, pat_ref, pw_ref, row_ref, col_ref = refs[:5]
    fine_ref, o_ref = refs[-2:]
    source = x_ref[...].astype(jnp.float32)
    lanes = source.shape[1]
    width = plan[0][0] * 0 + col_ref.shape[1]
    ext_rows = row_ref.shape[0]
    shifted = []
    for first in range(3):
        slab = pick_rows(source, ext_rows, 2 * first, source.shape[0])
        shifted.append(
            [slab if second == 0 else pltpu.roll(slab, lanes - 2 * second * chans, 1) for second in range(3)]
        )
    weight = pw_ref[...]
    parts = []
    for index in range(width // 128):
        window = slice(index * 128, (index + 1) * 128)
        total = None
        for first in range(3):
            for second in range(3):
                term = shifted[first][second][:, window] * pat_ref[3 * first + second : 3 * first + second + 1, :]
                total = term if total is None else total + term
        mixed = gelu_tanh(jnp.dot(total.astype(jnp.bfloat16), weight, preferred_element_type=jnp.float32))
        parts.append((shifted[1][1][:, window] + mixed).astype(jnp.bfloat16))
    hidden = jnp.concatenate(parts, axis=1)
    keep = row_ref[...] * col_ref[...]
    hidden = jnp.where(keep > 0, hidden, jnp.zeros_like(hidden)).astype(jnp.float32)
    inner = pltpu.roll(hidden, width - margin * chans, 1)[:, : cols * chans]
    fine_ref[...] = pick_rows(inner, rows, margin, ext_rows).astype(fine_ref.dtype)
    o_ref[...] = chain_levels(hidden, refs[5:-2], plan).astype(o_ref.dtype)


def chain_levels(value, refs, plan):
    lanes = value.shape[1]
    for level, (valid, rows, chans, outs) in enumerate(plan):
        near_ref, far_ref, w_ref = refs[3 * level : 3 + 3 * level]
        shape = (rows, value.shape[0])
        out_row = lax.broadcasted_iota(jnp.int32, shape, 0)
        in_row = lax.broadcasted_iota(jnp.int32, shape, 1)
        slabs = []
        for first in range(3):
            pick = ((in_row == 2 * out_row + first) & (in_row < valid)).astype(jnp.float32)
            slabs.append(jnp.dot(pick, value, preferred_element_type=jnp.float32))
        aheads = [pltpu.roll(slab, lanes - 2 * chans, 1) for slab in slabs]
        weight = w_ref[...]
        chunk = max(128, 2 * chans)
        width = weight.shape[1]
        parts = []
        for index in range(lanes // chunk):
            window = slice(index * chunk, (index + 1) * chunk)
            total = None
            for first in range(3):
                term = (
                    slabs[first][:, window] * near_ref[first : first + 1, :]
                    + aheads[first][:, window] * far_ref[first : first + 1, :]
                )
                total = term if total is None else total + term
            part = jnp.dot(total.astype(jnp.bfloat16), weight, preferred_element_type=jnp.float32)
            parts.append(gelu_tanh(part).astype(jnp.bfloat16))
        value = jnp.concatenate(parts, axis=1).astype(jnp.float32)
    return value


def chain_plan(rows, cols, chans, params):
    plan = []
    operands = []
    lanes = None
    for taps, weight in params:
        out_rows = (rows - 1) // 2
        out_cols = (cols - 1) // 2
        pairs = out_cols + 1
        if pairs * 2 * chans % 128:
            pairs += 1
        lanes = lanes or pairs * 2 * chans
        plan.append((rows, -(-out_rows // 8) * 8, chans, weight.shape[1]))
        operands.extend(prepare(taps, weight))
        rows, cols, chans = out_rows, out_cols, weight.shape[1]
    return tuple(plan), operands, lanes, (rows, cols, chans)


def strided_chain(ext, chans, params):
    rows = ext.shape[0]
    cols = ext.shape[1] // chans
    plan = []
    operands = []
    lanes = None
    for taps, weight in params:
        out_rows = (rows - 1) // 2
        out_cols = (cols - 1) // 2
        pairs = out_cols + 1
        if pairs * 2 * chans % 128:
            pairs += 1
        lanes = lanes or pairs * 2 * chans
        plan.append((rows, -(-out_rows // 8) * 8, chans, weight.shape[1]))
        operands.extend(prepare(taps, weight))
        rows, cols, chans = out_rows, out_cols, weight.shape[1]
    source = jnp.pad(ext, ((0, -ext.shape[0] % 8), (0, lanes - ext.shape[1])))
    result = pl.pallas_call(
        functools.partial(chain_kernel, plan=tuple(plan)),
        out_shape=jax.ShapeDtypeStruct((plan[-1][1], lanes), jnp.bfloat16),
    )(source, *operands)
    return result[:rows, : cols * chans]


def local(field, dw0, pw0, dw1, pw1, dw2, pw2, dw3, pw3, dw4, pw4, dwc, pwc):
    chans = dw0.shape[1]
    rows = field.shape[0]
    cols = field.shape[1] // chans
    depth = 4
    margin = 2**depth - 1
    upper = shifted(field[-margin - 2 :], "gx", 1)
    lower = shifted(field[:2], "gx", -1)
    stacked = jnp.concatenate([upper, field, lower], axis=0)
    params = ((dw1, pw1), (dw2, pw2), (dw3, pw3), (dw4, pw4))
    places = (lax.axis_index("gx"), lax.axis_index("gy"))
    (params, dw0, pw0, places), stacked = lax.optimization_barrier(((params, dw0, pw0, places), stacked))
    leftside = shifted(stacked[:, -(margin + 2) * chans :], "gy", 1)
    rightside = shifted(stacked[:, : 2 * chans], "gy", -1)
    flat_pad = jnp.concatenate([leftside, stacked, rightside], axis=1)
    ext_rows = rows + margin
    ext_cols = cols + margin
    plan, operands, lanes, (last_rows, last_cols, last_chans) = chain_plan(
        ext_rows, ext_cols, chans, params
    )
    padded_rows = -(-ext_rows // 8) * 8
    source = jnp.pad(
        flat_pad,
        (
            (0, padded_rows + 8 - flat_pad.shape[0]),
            (0, lanes + 128 - flat_pad.shape[1]),
        ),
    )
    pattern = jnp.tile(dw0, (1, 128 // chans))
    block = jnp.kron(jnp.eye(128 // chans, dtype=pw0.dtype), pw0)
    row_keep = (
        (places[0] > 0) | (lax.broadcasted_iota(jnp.int32, (padded_rows, 1), 0) >= margin)
    ).astype(jnp.float32)
    col_keep = (
        (places[1] > 0) | (lax.broadcasted_iota(jnp.int32, (1, lanes), 1) >= margin * chans)
    ).astype(jnp.float32)
    body = functools.partial(fine_kernel, plan=plan, rows=rows, cols=cols, margin=margin, chans=chans)
    fine, hidden = pl.pallas_call(
        body,
        out_shape=(
            jax.ShapeDtypeStruct((rows, cols * chans), jnp.bfloat16),
            jax.ShapeDtypeStruct((plan[-1][1], lanes), jnp.bfloat16),
        ),
    )(source, pattern, block, row_keep, col_keep, *operands)
    hidden = hidden[:last_rows, : last_cols * last_chans]
    coarse_chans = dwc.shape[2]
    halo = 2 ** (LC - 1) - 1
    grid4 = hidden.reshape(hidden.shape[0], -1, coarse_chans)
    upper = shifted(grid4[-1:], "gx", 1)
    extended = jnp.concatenate([upper, grid4], axis=0)
    leftside = shifted(extended[:, -halo:], "gy", 1)
    extended = jnp.concatenate([leftside, extended], axis=1)
    hidden = strided_cells(extended, dwc[0], pwc[0])
    hidden = lax.all_gather(hidden, "gx", axis=0, tiled=True)
    for level in range(1, LC - 1):
        hidden = strided_cells(pad_top(hidden), dwc[level], pwc[level])
    hidden = lax.all_gather(hidden, "gy", axis=1, tiled=True)
    hidden = strided_cells(pad_left(pad_top(hidden)), dwc[LC - 1], pwc[LC - 1])
    return (fine, hidden.reshape(hidden.shape[0], -1))


def pad_top(cells):
    return jnp.concatenate([jnp.zeros_like(cells[:1]), cells], axis=0)


def pad_left(cells):
    return jnp.concatenate([jnp.zeros_like(cells[:, :1]), cells], axis=1)


def strided_cells(padded, taps, weight):
    rows = (padded.shape[0] - 1) // 2
    cols = (padded.shape[1] - 1) // 2
    total = jnp.zeros((rows, cols, padded.shape[2]), jnp.float32)
    for first in range(3):
        for second in range(3):
            piece = padded[first : first + 2 * rows : 2, second : second + 2 * cols : 2]
            total = total + piece.astype(jnp.float32) * taps[3 * first + second]
    flat = total.astype(jnp.bfloat16).reshape(rows * cols, -1)
    mixed = jnp.dot(flat, weight, preferred_element_type=jnp.float32)
    return gelu_tanh(mixed).astype(jnp.bfloat16).reshape(rows, cols, weight.shape[1])


def solution(mesh):
    placed = (P("gx", "gy"), P(), P(), P(), P(), P(), P(), P(), P(), P(), P(), P(), P())
    return jax.shard_map(
        local, mesh=mesh, in_specs=placed, out_specs=(P("gx", "gy"), P()), check_vma=False
    )
```

```python
import functools

import numpy as np

import jax
import jax.numpy as jnp
from jax import lax
from jax.experimental import pallas as pl
from jax.experimental.pallas import tpu as pltpu
from jax.sharding import PartitionSpec as P

LC = 4


def shifted(value, axis, steps):
    count = lax.axis_size(axis)
    leading, last = (max(0, -steps), min(count, count - steps))
    return lax.ppermute(value, axis, [(source, source + steps) for source in range(leading, last)])


def padded_2(block, sides, width):
    for axis, dim in sides:
        count = lax.axis_size(axis)
        forward = [(i, i + 1) for i in range(count - 1)]
        backward = [(target, source) for source, target in forward]
        low = lax.ppermute(
            lax.slice_in_dim(block, block.shape[dim] - width, None, axis=dim), axis, forward
        )
        high = lax.ppermute(lax.slice_in_dim(block, 0, width, axis=dim), axis, backward)
        block = jnp.concatenate([low, block, high], axis=dim)
    return block


def gelu_tanh(value):
    return jax.nn.gelu(value, approximate=True)


def point_flat(spread, weight, rows, cols):
    chans = weight.shape[0]
    flat = spread.astype(jnp.bfloat16).reshape(rows * cols, chans)
    mixed = jnp.dot(flat, weight, preferred_element_type=jnp.float32)
    return gelu_tanh(mixed).reshape(rows, cols * weight.shape[1])


def down_level(field, taps, weight, split_rows, split_cols):
    chans = taps.shape[1]
    rows = field.shape[0]
    cols = field.shape[1] // chans
    half_rows = rows // 2
    half_cols = cols // 2
    if split_rows:
        upper = shifted(field[-1:], "gx", 1)
    else:
        upper = jnp.zeros((1, cols * chans), jnp.bfloat16)
    extended = jnp.concatenate([upper, field], axis=0)
    if split_cols:
        leftside = shifted(extended[:, -chans:], "gy", 1)
    else:
        leftside = jnp.zeros((rows + 1, chans), jnp.bfloat16)
    tiled = jnp.tile(taps, (1, half_cols))
    total = jnp.zeros((half_rows, half_cols * chans), jnp.float32)
    for first in range(3):
        slab = extended[first : first + rows : 2]
        left_slab = leftside[first : first + rows : 2]
        pairs = slab.reshape(half_rows, half_cols, 2 * chans)
        even_cells = pairs[:, :, :chans].reshape(half_rows, half_cols * chans)
        odd_cells = pairs[:, :, chans:].reshape(half_rows, half_cols * chans)
        before = jnp.concatenate([left_slab, odd_cells[:, :-chans]], axis=1)
        for second, piece in enumerate((before, even_cells, odd_cells)):
            total = total + piece.astype(jnp.float32) * tiled[3 * first + second]
    return point_flat(total, weight, half_rows, half_cols).astype(jnp.bfloat16)


def strided_flat(ext, taps, weight):
    chans = taps.shape[1]
    rows = (ext.shape[0] - 1) // 2
    cols = (ext.shape[1] // chans - 1) // 2
    tiled = jnp.tile(taps, (1, cols))
    total = jnp.zeros((rows, cols * chans), jnp.float32)
    for first in range(3):
        slab = ext[first : first + 2 * rows : 2]
        head = slab[:, : 2 * cols * chans].reshape(rows, cols, 2 * chans)
        tail = slab[:, chans:].reshape(rows, cols, 2 * chans)
        pieces = (head[:, :, :chans], head[:, :, chans:], tail[:, :, chans:])
        for second, piece in enumerate(pieces):
            piece = piece.reshape(rows, cols * chans)
            total = total + piece.astype(jnp.float32) * tiled[3 * first + second]
    return point_flat(total, weight, rows, cols).astype(jnp.bfloat16)


def prepare(taps, weight):
    chans = taps.shape[1]
    chunk = max(128, 2 * chans)
    group = chunk // (2 * chans)
    grouped = taps.reshape(3, 3, chans)
    near = jnp.tile(grouped[:, :2].reshape(3, 2 * chans), (1, group))
    far = jnp.tile(
        jnp.concatenate([grouped[:, 2:], jnp.zeros_like(grouped[:, 2:])], axis=1).reshape(3, 2 * chans),
        (1, group),
    )
    doubled = jnp.concatenate([weight, weight], axis=0)
    block = jnp.kron(jnp.eye(group, dtype=weight.dtype), doubled) if group > 1 else doubled
    return near, far, block


def chain_kernel(*refs, plan):
    value = refs[0][...].astype(jnp.float32)
    refs[-1][...] = chain_levels(value, refs[1:-1], plan).astype(refs[-1].dtype)


def pick_rows(value, rows, offset, valid):
    shape = (rows, value.shape[0])
    out_row = lax.broadcasted_iota(jnp.int32, shape, 0)
    in_row = lax.broadcasted_iota(jnp.int32, shape, 1)
    pick = ((in_row == offset + out_row) & (in_row < valid)).astype(jnp.float32)
    return jnp.dot(pick, value, preferred_element_type=jnp.float32)


def fine_kernel(x_ref, pats_ref, mats_ref, row_ref, col_ref, fine_ref, o_ref, *, plan, rows, cols, margin, chans, spots):
    pat_ref = pats_ref
    source = x_ref[...].astype(jnp.float32)
    lanes = source.shape[1]
    width = plan[0][0] * 0 + col_ref.shape[1]
    ext_rows = row_ref.shape[0]
    shifted = []
    for first in range(3):
        slab = pick_rows(source, ext_rows, 2 * first, source.shape[0])
        shifted.append(
            [slab if second == 0 else pltpu.roll(slab, lanes - 2 * second * chans, 1) for second in range(3)]
        )
    weight = mats_ref[0:128, 0:128]
    parts = []
    for index in range(width // 128):
        window = slice(index * 128, (index + 1) * 128)
        total = None
        for first in range(3):
            for second in range(3):
                tap = 3 * first + second
                term = shifted[first][second][:, window] * pat_ref[tap : tap + 1, 0:128]
                total = term if total is None else total + term
        mixed = gelu_tanh(jnp.dot(total.astype(jnp.bfloat16), weight, preferred_element_type=jnp.float32))
        parts.append((shifted[1][1][:, window] + mixed).astype(jnp.bfloat16))
    hidden = jnp.concatenate(parts, axis=1)
    keep = row_ref[...] * col_ref[...]
    hidden = jnp.where(keep > 0, hidden, jnp.zeros_like(hidden)).astype(jnp.float32)
    inner = pltpu.roll(hidden, width - margin * chans, 1)[:, : cols * chans]
    fine_ref[...] = pick_rows(inner, rows, margin, ext_rows).astype(fine_ref.dtype)
    o_ref[...] = chain_levels(hidden, (pats_ref, mats_ref, spots), plan).astype(o_ref.dtype)


def chain_levels(value, refs, plan):
    lanes = value.shape[1]
    for level, (valid, rows, chans, outs) in enumerate(plan):
        pats_ref, mats_ref, spots = refs
        row_at, mat_at, span, depth, across = spots[level]
        shape = (rows, value.shape[0])
        out_row = lax.broadcasted_iota(jnp.int32, shape, 0)
        in_row = lax.broadcasted_iota(jnp.int32, shape, 1)
        slabs = []
        for first in range(3):
            pick = ((in_row == 2 * out_row + first) & (in_row < valid)).astype(jnp.float32)
            slabs.append(jnp.dot(pick, value, preferred_element_type=jnp.float32))
        aheads = [pltpu.roll(slab, lanes - 2 * chans, 1) for slab in slabs]
        weight = mats_ref[mat_at : mat_at + depth, 0:across]
        chunk = max(128, 2 * chans)
        width = weight.shape[1]
        parts = []
        for index in range(lanes // chunk):
            window = slice(index * chunk, (index + 1) * chunk)
            total = None
            for first in range(3):
                near = pats_ref[row_at + first : row_at + first + 1, 0:span]
                far = pats_ref[row_at + 3 + first : row_at + 4 + first, 0:span]
                term = slabs[first][:, window] * near + aheads[first][:, window] * far
                total = term if total is None else total + term
            part = jnp.dot(total.astype(jnp.bfloat16), weight, preferred_element_type=jnp.float32)
            parts.append(gelu_tanh(part).astype(jnp.bfloat16))
        value = jnp.concatenate(parts, axis=1).astype(jnp.float32)
    return value


def chain_plan(rows, cols, chans, params):
    plan = []
    operands = []
    lanes = None
    for taps, weight in params:
        out_rows = (rows - 1) // 2
        out_cols = (cols - 1) // 2
        pairs = out_cols + 1
        if pairs * 2 * chans % 128:
            pairs += 1
        lanes = lanes or pairs * 2 * chans
        plan.append((rows, -(-out_rows // 8) * 8, chans, weight.shape[1]))
        operands.extend(prepare(taps, weight))
        rows, cols, chans = out_rows, out_cols, weight.shape[1]
    return tuple(plan), operands, lanes, (rows, cols, chans)


def strided_chain(ext, chans, params):
    rows = ext.shape[0]
    cols = ext.shape[1] // chans
    plan = []
    operands = []
    lanes = None
    for taps, weight in params:
        out_rows = (rows - 1) // 2
        out_cols = (cols - 1) // 2
        pairs = out_cols + 1
        if pairs * 2 * chans % 128:
            pairs += 1
        lanes = lanes or pairs * 2 * chans
        plan.append((rows, -(-out_rows // 8) * 8, chans, weight.shape[1]))
        operands.extend(prepare(taps, weight))
        rows, cols, chans = out_rows, out_cols, weight.shape[1]
    source = jnp.pad(ext, ((0, -ext.shape[0] % 8), (0, lanes - ext.shape[1])))
    result = pl.pallas_call(
        functools.partial(chain_kernel, plan=tuple(plan)),
        out_shape=jax.ShapeDtypeStruct((plan[-1][1], lanes), jnp.bfloat16),
    )(source, *operands)
    return result[:rows, : cols * chans]


def local(field, dw0, pw0, dw1, pw1, dw2, pw2, dw3, pw3, dw4, pw4, dwc, pwc):
    chans = dw0.shape[1]
    rows = field.shape[0]
    cols = field.shape[1] // chans
    depth = 4
    margin = 2**depth - 1
    upper = shifted(field[-margin - 2 :], "gx", 1)
    lower = shifted(field[:2], "gx", -1)
    stacked = jnp.concatenate([upper, field, lower], axis=0)
    params = ((dw1, pw1), (dw2, pw2), (dw3, pw3), (dw4, pw4))
    places = (lax.axis_index("gx"), lax.axis_index("gy"))
    (params, dw0, pw0, places), stacked = lax.optimization_barrier(((params, dw0, pw0, places), stacked))
    leftside = shifted(stacked[:, -(margin + 2) * chans :], "gy", 1)
    rightside = shifted(stacked[:, : 2 * chans], "gy", -1)
    flat_pad = jnp.concatenate([leftside, stacked, rightside], axis=1)
    ext_rows = rows + margin
    ext_cols = cols + margin
    plan, operands, lanes, (last_rows, last_cols, last_chans) = chain_plan(
        ext_rows, ext_cols, chans, params
    )
    padded_rows = -(-ext_rows // 8) * 8
    source = jnp.pad(
        flat_pad,
        (
            (0, padded_rows + 8 - flat_pad.shape[0]),
            (0, lanes + 128 - flat_pad.shape[1]),
        ),
    )
    pattern = jnp.tile(dw0, (1, 128 // chans))
    block = jnp.kron(jnp.eye(128 // chans, dtype=pw0.dtype), pw0)
    span = max(piece.shape[1] for piece in operands)
    taps_all = [dw0] + [taps for taps, _ in params]
    flat_taps = jnp.concatenate([taps.reshape(-1) for taps in taps_all] + [jnp.zeros((1,), dw0.dtype)])
    zero_at = flat_taps.shape[0] - 1
    index = np.full((9 + 6 * len(plan), span), zero_at, np.int32)
    lane = np.arange(span)
    index[:9, :128] = np.arange(9)[:, None] * chans + lane[None, :128] % chans
    mat_rows = [block]
    spots = []
    row_at, mat_at, base = 9, 128, dw0.size
    for level, (taps, _) in enumerate(params):
        width = taps.shape[1]
        mat = operands[3 * level + 2]
        chunk = max(128, 2 * width)
        inner = lane[:chunk] % (2 * width)
        for first in range(3):
            index[row_at + first, :chunk] = base + (3 * first + inner // width) * width + inner % width
            far = np.where(inner < width, base + (3 * first + 2) * width + inner % width, zero_at)
            index[row_at + 3 + first, :chunk] = far
        mat_rows.append(mat)
        spots.append((row_at, mat_at, chunk, mat.shape[0], mat.shape[1]))
        row_at += 6
        mat_at += mat.shape[0]
        base += taps.size
    pats = flat_taps[jnp.asarray(index)]
    mats = jnp.concatenate(
        [jnp.pad(piece, ((0, 0), (0, span - piece.shape[1]))) for piece in mat_rows], axis=0
    )
    row_keep = (
        (places[0] > 0) | (lax.broadcasted_iota(jnp.int32, (padded_rows, 1), 0) >= margin)
    ).astype(jnp.float32)
    col_keep = (
        (places[1] > 0) | (lax.broadcasted_iota(jnp.int32, (1, lanes), 1) >= margin * chans)
    ).astype(jnp.float32)
    body = functools.partial(
        fine_kernel, plan=plan, rows=rows, cols=cols, margin=margin, chans=chans, spots=tuple(spots)
    )
    fine, hidden = pl.pallas_call(
        body,
        out_shape=(
            jax.ShapeDtypeStruct((rows, cols * chans), jnp.bfloat16),
            jax.ShapeDtypeStruct((plan[-1][1], lanes), jnp.bfloat16),
        ),
    )(source, pats, mats, row_keep, col_keep)
    hidden = hidden[:last_rows, : last_cols * last_chans]
    coarse_chans = dwc.shape[2]
    halo = 2 ** (LC - 1) - 1
    grid4 = hidden.reshape(hidden.shape[0], -1, coarse_chans)
    upper = shifted(grid4[-1:], "gx", 1)
    extended = jnp.concatenate([upper, grid4], axis=0)
    leftside = shifted(extended[:, -halo:], "gy", 1)
    extended = jnp.concatenate([leftside, extended], axis=1)
    hidden = strided_cells(extended, dwc[0], pwc[0])
    hidden = lax.all_gather(hidden, "gx", axis=0, tiled=True)
    for level in range(1, LC - 1):
        hidden = strided_cells(pad_top(hidden), dwc[level], pwc[level])
    hidden = lax.all_gather(hidden, "gy", axis=1, tiled=True)
    hidden = strided_cells(pad_left(pad_top(hidden)), dwc[LC - 1], pwc[LC - 1])
    return (fine, hidden.reshape(hidden.shape[0], -1))


def pad_top(cells):
    return jnp.concatenate([jnp.zeros_like(cells[:1]), cells], axis=0)


def pad_left(cells):
    return jnp.concatenate([jnp.zeros_like(cells[:, :1]), cells], axis=1)


def strided_cells(padded, taps, weight):
    rows = (padded.shape[0] - 1) // 2
    cols = (padded.shape[1] - 1) // 2
    total = jnp.zeros((rows, cols, padded.shape[2]), jnp.float32)
    for first in range(3):
        for second in range(3):
            piece = padded[first : first + 2 * rows : 2, second : second + 2 * cols : 2]
            total = total + piece.astype(jnp.float32) * taps[3 * first + second]
    flat = total.astype(jnp.bfloat16).reshape(rows * cols, -1)
    mixed = jnp.dot(flat, weight, preferred_element_type=jnp.float32)
    return gelu_tanh(mixed).astype(jnp.bfloat16).reshape(rows, cols, weight.shape[1])


def solution(mesh):
    placed = (P("gx", "gy"), P(), P(), P(), P(), P(), P(), P(), P(), P(), P(), P(), P())
    return jax.shard_map(
        local, mesh=mesh, in_specs=placed, out_specs=(P("gx", "gy"), P()), check_vma=False
    )
```
